32 devices in a mesh: seq: 4 (over z), crow: 4 (over y, x), ccol: 2 (over core).
Axes of the slice: x: 2, y: 2, z: 4, core: 2. Of those that a mesh axis runs over, the one named last changes fastest.
Arguments:
- features: float32 [8, 768, 1024], P(None, ('crow', 'ccol'), 'seq'), may hold values from -6 to 6
- first_channel_scale: float32 [768], P(('crow', 'ccol')), may hold values from 0.5 to 2
- first_channel_shift: float32 [768], P(('crow', 'ccol')), may hold values from -3 to 3
- first_conv_bias: float32 [768], P(('crow', 'ccol')), may hold values from -3 to 3
- first_kernel_taps: float32 [5, 768, 768], P(None, ('crow', 'ccol')), may hold values from -0.09375 to 0.09375
- second_channel_scale: float32 [768], P(('crow', 'ccol')), may hold values from 0.5 to 2
- second_channel_shift: float32 [768], P(('crow', 'ccol')), may hold values from -3 to 3
- second_conv_bias: float32 [768], P(('crow', 'ccol')), may hold values from -3 to 3
- second_kernel_taps: float32 [5, 768, 768], P(None, ('crow', 'ccol')), may hold values from -0.09375 to 0.09375
- up_weight: float32 [1536, 768], P(('crow', 'ccol')), may hold values from -0.21875 to 0.21875
- norm_gain: float32 [1536], replicated, may hold values from 0.5 to 2
- qkv_weight: float32 [1536, 4608], P(None, ('crow', 'ccol')), as said below
- out_weight: float32 [1536, 1536], P(('crow', 'ccol')), may hold values from -0.625 to 0.625
Outputs:
- tower_skip_output: float32 [8, 768, 1024], P(None, ('crow', 'ccol'), 'seq')
- attended: float32 [8, 128, 1536], P(None, 'seq', ('crow', 'ccol'))
The draws below stay inside these ranges and needn't reach their ends.
Inputs may be any that keep to these rules, and one draw needn't show every extreme that they name: `qkv_weight`: entries are of order 1 / sqrt(1536) times a few.
All inputs are finite; a program needn't handle non-finite values.
Results may differ from the reference program's by a relative error of at most 0.0003.
Values sent between devices are 32-bit elements; how exact they have to be, the bound alone decides.
No kernel may reach another device: no remote copies, remote signals or barrier semaphores. Data moves between devices by JAX's collectives and lax.ppermute only.
A program may use at most 192 MiB of HBM per device.

```python
import math
import jax
import jax.numpy as jnp
from jax import lax

C = 768
CA = 1536
HEADS = 8
HEAD_SIZE = 192
TAPS = 5
FIRST_DILATION = 2
SECOND_DILATION = 4
POOL = 8
BATCH = 8
L16 = 1024
L128 = 128


def draw_qkv_weight(key, part):
    keys = jax.random.split(jax.random.fold_in(key, 7), 1)
    base = jax.random.truncated_normal(keys[0], -4.0, 4.0, (CA, HEADS, 3, HEAD_SIZE), jnp.float32) * (2.0 / math.sqrt(CA))
    return base.reshape(CA, 3 * CA)


def with_spikes(entries, stream_key, source, target, parts, factor):
    owner, partner = [(jnp.arange(entries.shape[position]) // (entries.shape[position] // parts)).reshape([-1 if axis == position else 1 for axis in range(entries.ndim)]) for position in (source, target)]
    chosen = jax.random.permutation(stream_key, parts)[partner]
    strong = (owner == chosen) | (owner == (partner + parts // 2) % parts)
    return jnp.where(strong, factor * entries, entries)


def shard_levels(stream_key, shape, cuts, low, high):
    def one(dim, blocks):
        draws = jax.random.uniform(jax.random.fold_in(jax.random.fold_in(stream_key, 6), dim), (blocks,), jnp.float32, low / len(cuts), high / len(cuts))
        return jnp.repeat(jnp.exp(draws), shape[dim] // blocks).reshape((-1,) + (1,) * (len(shape) - dim - 1))

    factor_of = one(*cuts[0])
    for cut in cuts[1:]:
        factor_of = factor_of * one(*cut)
    return factor_of


def gaussian(key, extent, scale, bound, cuts=(), held_as=jnp.bfloat16):
    gain = shard_levels(key, extent, cuts, -0.22, 0.18) if cuts else 1.0
    result = jax.random.normal(key, extent, jnp.float32) * scale * gain
    return jnp.minimum(jnp.maximum(result, -bound), bound).astype(held_as)


def bell_draw_with(key, dims, deviation, bound, shards, heavy, dtype=jnp.bfloat16):
    values = deviation * jax.random.normal(key, dims, jnp.float32)
    if shards:
        values = values * shard_levels(key, dims, shards, -0.22, 0.18)
    return jnp.clip(with_spikes(values, jax.random.fold_in(key, 3), *heavy), -bound, bound).astype(dtype)


def setup_inputs(seed: int = 0) -> dict:
    streams_of = jax.random.split(jax.random.key(seed), 14)
    return {
        "features": gaussian(streams_of[0], (BATCH, C, L16), 1.0, 6.0, ((1, 8), (2, 4)), jnp.float32),
        "first_channel_scale": jnp.clip(jnp.exp(math.log(2.0) - 1.3862944 * jax.random.uniform(streams_of[1], (C,), jnp.float32) ** shard_levels(streams_of[1], (C,), ((0, 8),), -0.2, 0.2)), 0.5, 2.0),
        "first_channel_shift": gaussian(streams_of[2], (C,), 0.5, 3.0, ((0, 8),), jnp.float32),
        "first_conv_bias": gaussian(streams_of[3], (C,), 0.5, 3.0, ((0, 8),), jnp.float32),
        "first_kernel_taps": gaussian(streams_of[4], (TAPS, C, C), (TAPS * C) ** -0.5, 0.09375, ((1, 8),), jnp.float32),
        "second_channel_scale": jnp.clip(jnp.exp(math.log(2.0) - 1.3862944 * jax.random.uniform(streams_of[5], (C,), jnp.float32) ** shard_levels(streams_of[5], (C,), ((0, 8),), -0.2, 0.2)), 0.5, 2.0),
        "second_channel_shift": gaussian(streams_of[6], (C,), 0.5, 3.0, ((0, 8),), jnp.float32),
        "second_conv_bias": gaussian(streams_of[7], (C,), 0.5, 3.0, ((0, 8),), jnp.float32),
        "second_kernel_taps": gaussian(streams_of[8], (TAPS, C, C), (TAPS * C) ** -0.5, 0.09375, ((1, 8),), jnp.float32),
        "up_weight": gaussian(streams_of[9], (CA, C), C ** -0.5, 0.21875, ((0, 8),), jnp.float32),
        "norm_gain": jnp.clip(jnp.exp(jax.random.uniform(streams_of[10], (CA,), jnp.float32, math.log(0.5), math.log(2.0))), 0.5, 2.0),
        "qkv_weight": draw_qkv_weight(jax.random.fold_in(streams_of[13], 71), 0),
        "out_weight": bell_draw_with(streams_of[12], (CA, CA), HEAD_SIZE ** -0.5, 0.625, ((0, 8),), (0, 1, 8, 2.0), jnp.float32),
    }


HIGH_PRECISION = lax.Precision.HIGHEST

def convolution_layer(inputs, bn_scale, bn_shift, conv_bias, kernel, dilation):
    activated = jax.nn.gelu(inputs * bn_scale + bn_shift, approximate=False)
    row_count = inputs.shape[1]
    padded = jnp.pad(activated, ((0, 0), (2 * dilation, 2 * dilation), (0, 0)))
    summed = jnp.zeros(inputs.shape, jnp.float32)
    for tap_index in range(TAPS):
        window = padded[:, tap_index * dilation:tap_index * dilation + row_count, :]
        summed = summed + jnp.einsum('btc,oc->bto', window, kernel[tap_index], precision=HIGH_PRECISION)
    return inputs + summed + conv_bias

def rotate(values, positions):
    half_width = values.shape[-1] // 2
    frequency = jnp.exp(-math.log(10000.0) * jnp.arange(half_width).astype(jnp.float32) / half_width)
    angle = positions[:, None] * frequency[None, :]
    cosine = jnp.cos(angle)
    sine_part = jnp.sin(angle)
    lower_half = values[..., :half_width]
    upper_half = values[..., half_width:]
    return jnp.concatenate([lower_half * cosine - upper_half * sine_part, lower_half * sine_part + upper_half * cosine], axis=-1)

def reference(features, first_channel_scale, first_channel_shift, first_conv_bias, first_kernel_taps, second_channel_scale, second_channel_shift, second_conv_bias, second_kernel_taps, up_weight, norm_gain, qkv_weight, out_weight):
    rows_trailing = jnp.transpose(features, (0, 2, 1))
    first_part = convolution_layer(rows_trailing, first_channel_scale, first_channel_shift, first_conv_bias, first_kernel_taps, FIRST_DILATION)
    dilated_tower = convolution_layer(first_part, second_channel_scale, second_channel_shift, second_conv_bias, second_kernel_taps, SECOND_DILATION)
    tower_skip_output = jnp.transpose(dilated_tower, (0, 2, 1))
    batch_count = features.shape[0]
    pooled = lax.optimization_barrier(jnp.max(dilated_tower.reshape(batch_count, L128, POOL, C), axis=2))
    hidden = jnp.einsum('btc,oc->bto', pooled, up_weight, precision=HIGH_PRECISION)
    root_mean = jnp.sqrt(lax.optimization_barrier(jnp.mean(hidden * hidden, axis=2, keepdims=True)) + 1e-06)
    normed = hidden / root_mean * norm_gain
    positions = jnp.arange(L128).astype(jnp.float32)
    head_weights = jnp.transpose(qkv_weight.reshape(CA, HEADS, 3 * HEAD_SIZE), (1, 0, 2))
    head_outputs = out_weight.reshape(HEADS, HEAD_SIZE, CA)

    def one_head(running_total, pair):
        head_weight, head_output = pair
        projected = jnp.einsum('btc,co->bto', normed, head_weight, precision=HIGH_PRECISION)
        query_rows = rotate(projected[..., :HEAD_SIZE], positions)
        key_matrix = rotate(projected[..., HEAD_SIZE:2 * HEAD_SIZE], positions)
        value_matrix = projected[..., 2 * HEAD_SIZE:]
        attention_scores = jnp.einsum('jnc,jxc->jnx', query_rows, key_matrix, precision=HIGH_PRECISION) / math.sqrt(HEAD_SIZE)
        probabilities = jax.nn.softmax(attention_scores, axis=-1)
        weighted_values = jnp.einsum('zsv,zve->zse', probabilities, value_matrix, precision=HIGH_PRECISION)
        return (running_total + jnp.einsum('ivt,ts->ivs', weighted_values, head_output, precision=HIGH_PRECISION), None)
    initial = jnp.zeros((batch_count, L128, CA), jnp.float32)
    attended, _ = lax.scan(one_head, initial, (head_weights, head_outputs))
    return (tower_skip_output, attended)
```

```python
import math

import jax
import jax.numpy as jnp
from jax import lax
from jax.sharding import PartitionSpec as P

FIRST_DILATION = 2
SECOND_DILATION = 4
POOL = 8
TAPS = 5

MATMUL_PRECISION = lax.Precision.HIGH
CHANNELS = ("crow", "ccol")


def gathered(x, axis_name):
    count = lax.axis_size(axis_name)
    copies = jnp.broadcast_to(x[None], (count,) + x.shape)
    return lax.all_to_all(copies, axis_name, 0, 0, tiled=True)


def summed_scatter(x, axis_name):
    return jnp.sum(lax.all_to_all(x, axis_name, 0, 0, tiled=True), axis=0)


def swap_ccol(x):
    return lax.ppermute(x, "ccol", [(0, 1), (1, 0)])


def shifted_in(edge, forward):
    count = lax.axis_size("seq")
    if forward:
        pairs = [(i, i + 1) for i in range(count - 1)]
    else:
        pairs = [(i + 1, i) for i in range(count - 1)]
    return lax.ppermute(edge, "seq", pairs)


def convolution_block(inputs, bn_scale, bn_shift, conv_bias, kernel, dilation):
    activated = jax.nn.gelu(inputs * bn_scale[:, None] + bn_shift[:, None], approximate=False)
    by_row = gathered(activated, "crow")
    other_core = swap_ccol(by_row)
    core = lax.axis_index("ccol")
    blocks = jnp.where(core == 0, jnp.stack([by_row, other_core]), jnp.stack([other_core, by_row]))
    width = 2 * dilation
    rows = inputs.shape[2]
    left_edge = jnp.swapaxes(blocks[..., :width], -1, -2)
    right_edge = jnp.swapaxes(blocks[..., rows - width :], -1, -2)
    left_halo = jnp.swapaxes(shifted_in(right_edge, True), -1, -2)
    right_halo = jnp.swapaxes(shifted_in(left_edge, False), -1, -2)
    extended = jnp.concatenate([left_halo, blocks, right_halo], axis=-1)
    tap_count, out_count, in_count = kernel.shape
    row_count = lax.axis_size("crow")
    block = in_count // (2 * row_count)
    weights = kernel.reshape(tap_count, out_count, row_count, 2, block)
    summed = None
    for tap_index in range(tap_count):
        window = extended[..., tap_index * dilation : tap_index * dilation + rows]
        term = jnp.einsum(
            "krbit,orki->bot", window, weights[tap_index], precision=MATMUL_PRECISION
        )
        summed = term if summed is None else summed + term
    return inputs + summed + conv_bias[:, None]


def rotate(values, positions):
    half_width = values.shape[-1] // 2
    frequency = jnp.exp(
        -math.log(10000.0) * jnp.arange(half_width).astype(jnp.float32) / half_width
    )
    angle = positions[:, None] * frequency[None, :]
    cosine = jnp.cos(angle)
    sine_part = jnp.sin(angle)
    lower_half = values[..., :half_width]
    upper_half = values[..., half_width:]
    return jnp.concatenate(
        [
            lower_half * cosine - upper_half * sine_part,
            lower_half * sine_part + upper_half * cosine,
        ],
        axis=-1,
    )


def per_device(
    features,
    first_channel_scale,
    first_channel_shift,
    first_conv_bias,
    first_kernel_taps,
    second_channel_scale,
    second_channel_shift,
    second_conv_bias,
    second_kernel_taps,
    up_weight,
    norm_gain,
    qkv_weight,
    out_weight,
):
    batch_count = features.shape[0]
    channels = features.shape[1]
    row_count = features.shape[2]
    first_part = convolution_block(
        features,
        first_channel_scale,
        first_channel_shift,
        first_conv_bias,
        first_kernel_taps,
        FIRST_DILATION,
    )
    tower_skip_output = convolution_block(
        first_part,
        second_channel_scale,
        second_channel_shift,
        second_conv_bias,
        second_kernel_taps,
        SECOND_DILATION,
    )
    pooled_rows = row_count // POOL
    pooled = jnp.transpose(
        jnp.max(tower_skip_output.reshape(batch_count, channels, pooled_rows, POOL), axis=3),
        (0, 2, 1),
    )
    group = lax.axis_size(CHANNELS)
    pooled_all = gathered(pooled, CHANNELS)
    up_blocks = up_weight.reshape(up_weight.shape[0], group, channels)
    hidden = jnp.einsum("nbti,oni->bto", pooled_all, up_blocks, precision=MATMUL_PRECISION)
    hidden_all = gathered(hidden, CHANNELS)
    attn_width = norm_gain.shape[0]
    squares = jnp.sum(hidden_all * hidden_all, axis=(0, 3))
    gain_blocks = norm_gain.reshape(group, 1, 1, attn_width // group)
    qkv_blocks = qkv_weight.reshape(group, attn_width // group, qkv_weight.shape[1])
    projected = jnp.einsum(
        "nbtj,njo->bto", hidden_all * gain_blocks, qkv_blocks, precision=MATMUL_PRECISION
    )
    root_mean = jnp.sqrt(squares / attn_width + 1e-06)
    projected = projected / root_mean[..., None]
    head_extent = qkv_weight.shape[1] // 3
    positions = (
        lax.axis_index("seq") * pooled_rows + jnp.arange(pooled_rows, dtype=jnp.int32)
    ).astype(jnp.float32)
    query_rows = rotate(projected[..., :head_extent], positions) / math.sqrt(head_extent)
    key_matrix = rotate(projected[..., head_extent : 2 * head_extent], positions)
    keys_and_values = jnp.concatenate([key_matrix, projected[..., 2 * head_extent :]], axis=2)
    kv_all = gathered(keys_and_values, "seq")
    attention_scores = jnp.einsum(
        "btc,nbxc->btnx", query_rows, kv_all[..., :head_extent], precision=MATMUL_PRECISION
    )
    top = jnp.max(attention_scores, axis=(2, 3))
    probabilities = jnp.exp(attention_scores - top[..., None, None])
    denominator = jnp.sum(probabilities, axis=(2, 3))
    weighted_values = jnp.einsum(
        "btnx,nbxe->bte", probabilities, kv_all[..., head_extent:], precision=MATMUL_PRECISION
    )
    head_result = weighted_values / denominator[..., None]
    out_blocks = out_weight.reshape(out_weight.shape[0], group, out_weight.shape[1] // group)
    shares = jnp.einsum("btd,dne->nbte", head_result, out_blocks, precision=MATMUL_PRECISION)
    attended = summed_scatter(shares, CHANNELS)
    return (tower_skip_output, attended)


def solution(mesh):
    placed = (
        P(None, CHANNELS, "seq"),
        P(CHANNELS),
        P(CHANNELS),
        P(CHANNELS),
        P(None, CHANNELS, None),
        P(CHANNELS),
        P(CHANNELS),
        P(CHANNELS),
        P(None, CHANNELS, None),
        P(CHANNELS, None),
        P(),
        P(None, CHANNELS),
        P(CHANNELS, None),
    )
    return jax.shard_map(
        per_device,
        mesh=mesh,
        in_specs=placed,
        out_specs=(P(None, CHANNELS, "seq"), P(None, "seq", CHANNELS)),
        check_vma=False,
    )
```

```python
import math

import jax
import jax.numpy as jnp
from jax import lax
from jax.sharding import PartitionSpec as P

FIRST_DILATION = 2
SECOND_DILATION = 4
POOL = 8
TAPS = 5

MATMUL_PRECISION = lax.Precision.HIGH
CHANNELS = ("crow", "ccol")


def gathered(x, axis_name):
    count = lax.axis_size(axis_name)
    copies = jnp.broadcast_to(x[None], (count,) + x.shape)
    return lax.all_to_all(copies, axis_name, 0, 0, tiled=True)


def summed_scatter(x, axis_name):
    return jnp.sum(lax.all_to_all(x, axis_name, 0, 0, tiled=True), axis=0)


def swap_ccol(x):
    return lax.ppermute(x, "ccol", [(0, 1), (1, 0)])


def shifted_in(edge, forward):
    count = lax.axis_size("seq")
    if forward:
        pairs = [(i, i + 1) for i in range(count - 1)]
    else:
        pairs = [(i + 1, i) for i in range(count - 1)]
    return lax.ppermute(edge, "seq", pairs)


def convolution_block(inputs, bn_scale, bn_shift, conv_bias, kernel, dilation):
    activated = jax.nn.gelu(inputs * bn_scale[:, None] + bn_shift[:, None], approximate=False)
    by_row = gathered(activated, "crow")
    other_core = swap_ccol(by_row)
    core = lax.axis_index("ccol")
    tap_count, out_count, in_count = kernel.shape
    row_count = lax.axis_size("crow")
    block = in_count // (2 * row_count)
    weights = jnp.transpose(kernel.reshape(tap_count * out_count, in_count))
    weights = weights.reshape(row_count, 2, block, tap_count * out_count)
    own_weights = lax.dynamic_index_in_dim(weights, core, axis=1, keepdims=False)
    other_weights = lax.dynamic_index_in_dim(weights, 1 - core, axis=1, keepdims=False)
    products = jnp.einsum(
        "rbit,rio->bot", by_row, own_weights, precision=MATMUL_PRECISION
    ) + jnp.einsum("rbit,rio->bot", other_core, other_weights, precision=MATMUL_PRECISION)
    batch_count, rows = inputs.shape[0], inputs.shape[2]
    products = products.reshape(batch_count, tap_count, out_count, rows)
    width = 2 * dilation
    padded = jnp.pad(products, ((0, 0), (0, 0), (0, 0), (2 * width, 2 * width)))
    spread = None
    for tap_index in range(tap_count):
        offset = tap_index * dilation
        term = padded[:, tap_index, :, offset : offset + rows + 2 * width]
        spread = term if spread is None else spread + term
    to_left = jnp.swapaxes(spread[..., :width], 1, 2)
    to_right = jnp.swapaxes(spread[..., rows + width :], 1, 2)
    from_left = jnp.swapaxes(shifted_in(to_right, True), 1, 2)
    from_right = jnp.swapaxes(shifted_in(to_left, False), 1, 2)
    edges = jnp.concatenate(
        [from_left, jnp.zeros((batch_count, out_count, rows - 2 * width), jnp.float32), from_right],
        axis=2,
    )
    summed = spread[..., width : width + rows] + edges
    return inputs + summed + conv_bias[:, None]


def rotate(values, positions):
    half_width = values.shape[-1] // 2
    frequency = jnp.exp(
        -math.log(10000.0) * jnp.arange(half_width).astype(jnp.float32) / half_width
    )
    angle = positions[:, None] * frequency[None, :]
    cosine = jnp.cos(angle)
    sine_part = jnp.sin(angle)
    lower_half = values[..., :half_width]
    upper_half = values[..., half_width:]
    return jnp.concatenate(
        [
            lower_half * cosine - upper_half * sine_part,
            lower_half * sine_part + upper_half * cosine,
        ],
        axis=-1,
    )


def per_device(
    features,
    first_channel_scale,
    first_channel_shift,
    first_conv_bias,
    first_kernel_taps,
    second_channel_scale,
    second_channel_shift,
    second_conv_bias,
    second_kernel_taps,
    up_weight,
    norm_gain,
    qkv_weight,
    out_weight,
):
    batch_count = features.shape[0]
    channels = features.shape[1]
    row_count = features.shape[2]
    first_part = convolution_block(
        features,
        first_channel_scale,
        first_channel_shift,
        first_conv_bias,
        first_kernel_taps,
        FIRST_DILATION,
    )
    tower_skip_output = convolution_block(
        first_part,
        second_channel_scale,
        second_channel_shift,
        second_conv_bias,
        second_kernel_taps,
        SECOND_DILATION,
    )
    pooled_rows = row_count // POOL
    pooled = jnp.transpose(
        jnp.max(tower_skip_output.reshape(batch_count, channels, pooled_rows, POOL), axis=3),
        (0, 2, 1),
    )
    group = lax.axis_size(CHANNELS)
    pooled_all = gathered(pooled, CHANNELS)
    up_blocks = up_weight.reshape(up_weight.shape[0], group, channels)
    hidden = jnp.einsum("nbti,oni->bto", pooled_all, up_blocks, precision=MATMUL_PRECISION)
    hidden_all = gathered(hidden, CHANNELS)
    attn_width = norm_gain.shape[0]
    squares = jnp.sum(hidden_all * hidden_all, axis=(0, 3))
    gain_blocks = norm_gain.reshape(group, 1, 1, attn_width // group)
    qkv_blocks = qkv_weight.reshape(group, attn_width // group, qkv_weight.shape[1])
    projected = jnp.einsum(
        "nbtj,njo->bto", hidden_all * gain_blocks, qkv_blocks, precision=MATMUL_PRECISION
    )
    root_mean = jnp.sqrt(squares / attn_width + 1e-06)
    projected = projected / root_mean[..., None]
    head_extent = qkv_weight.shape[1] // 3
    positions = (
        lax.axis_index("seq") * pooled_rows + jnp.arange(pooled_rows, dtype=jnp.int32)
    ).astype(jnp.float32)
    query_rows = rotate(projected[..., :head_extent], positions) / math.sqrt(head_extent)
    key_matrix = rotate(projected[..., head_extent : 2 * head_extent], positions)
    keys_and_values = jnp.concatenate([key_matrix, projected[..., 2 * head_extent :]], axis=2)
    kv_all = gathered(keys_and_values, "seq")
    attention_scores = jnp.einsum(
        "btc,nbxc->btnx", query_rows, kv_all[..., :head_extent], precision=MATMUL_PRECISION
    )
    top = jnp.max(attention_scores, axis=(2, 3))
    probabilities = jnp.exp(attention_scores - top[..., None, None])
    denominator = jnp.sum(probabilities, axis=(2, 3))
    weighted_values = jnp.einsum(
        "btnx,nbxe->bte", probabilities, kv_all[..., head_extent:], precision=MATMUL_PRECISION
    )
    head_result = weighted_values / denominator[..., None]
    out_blocks = out_weight.reshape(out_weight.shape[0], group, out_weight.shape[1] // group)
    shares = jnp.einsum("btd,dne->nbte", head_result, out_blocks, precision=MATMUL_PRECISION)
    attended = summed_scatter(shares, CHANNELS)
    return (tower_skip_output, attended)


def solution(mesh):
    placed = (
        P(None, CHANNELS, "seq"),
        P(CHANNELS),
        P(CHANNELS),
        P(CHANNELS),
        P(None, CHANNELS, None),
        P(CHANNELS),
        P(CHANNELS),
        P(CHANNELS),
        P(None, CHANNELS, None),
        P(CHANNELS, None),
        P(),
        P(None, CHANNELS),
        P(CHANNELS, None),
    )
    return jax.shard_map(
        per_device,
        mesh=mesh,
        in_specs=placed,
        out_specs=(P(None, CHANNELS, "seq"), P(None, "seq", CHANNELS)),
        check_vma=False,
    )
```

```python
import math

import jax
import jax.numpy as jnp
from jax import lax
from jax.sharding import PartitionSpec as P

FIRST_DILATION = 2
SECOND_DILATION = 4
POOL = 8
TAPS = 5

MATMUL_PRECISION = lax.Precision.HIGH
CHANNELS = ("crow", "ccol")


def gathered(x, axis_name):
    count = lax.axis_size(axis_name)
    copies = jnp.broadcast_to(x[None], (count,) + x.shape)
    return lax.all_to_all(copies, axis_name, 0, 0, tiled=True)


def summed_scatter(x, axis_name):
    return jnp.sum(lax.all_to_all(x, axis_name, 0, 0, tiled=True), axis=0)


def swap_ccol(x):
    return lax.ppermute(x, "ccol", [(0, 1), (1, 0)])


def shifted_in(edge, forward):
    count = lax.axis_size("seq")
    if forward:
        pairs = [(i, i + 1) for i in range(count - 1)]
    else:
        pairs = [(i + 1, i) for i in range(count - 1)]
    return lax.ppermute(edge, "seq", pairs)


def convolution_block(inputs, bn_scale, bn_shift, conv_bias, kernel, dilation):
    activated = jax.nn.gelu(inputs * bn_scale[:, None] + bn_shift[:, None], approximate=False)
    by_row = gathered(activated, "crow")
    other_core = swap_ccol(by_row)
    core = lax.axis_index("ccol")
    tap_count, out_count, in_count = kernel.shape
    row_count = lax.axis_size("crow")
    block = in_count // (2 * row_count)
    weights = jnp.transpose(kernel.reshape(tap_count * out_count, in_count))
    weights = weights.reshape(row_count, 2, block, tap_count * out_count)
    own_weights = lax.dynamic_index_in_dim(weights, core, axis=1, keepdims=False)
    other_weights = lax.dynamic_index_in_dim(weights, 1 - core, axis=1, keepdims=False)
    products = jnp.einsum(
        "rbit,rio->bot", by_row, own_weights, precision=MATMUL_PRECISION
    ) + jnp.einsum("rbit,rio->bot", other_core, other_weights, precision=MATMUL_PRECISION)
    batch_count, rows = inputs.shape[0], inputs.shape[2]
    products = products.reshape(batch_count, tap_count, out_count, rows)
    width = 2 * dilation
    padded = jnp.pad(products, ((0, 0), (0, 0), (0, 0), (2 * width, 2 * width)))
    spread = None
    for tap_index in range(tap_count):
        offset = tap_index * dilation
        term = padded[:, tap_index, :, offset : offset + rows + 2 * width]
        spread = term if spread is None else spread + term
    to_left = jnp.swapaxes(spread[..., :width], 1, 2)
    to_right = jnp.swapaxes(spread[..., rows + width :], 1, 2)
    from_left = jnp.swapaxes(shifted_in(to_right, True), 1, 2)
    from_right = jnp.swapaxes(shifted_in(to_left, False), 1, 2)
    edges = jnp.concatenate(
        [from_left, jnp.zeros((batch_count, out_count, rows - 2 * width), jnp.float32), from_right],
        axis=2,
    )
    summed = spread[..., width : width + rows] + edges
    return inputs + summed + conv_bias[:, None]


def rotate(values, positions):
    half_width = values.shape[-1] // 2
    frequency = jnp.exp(
        -math.log(10000.0) * jnp.arange(half_width).astype(jnp.float32) / half_width
    )
    angle = positions[:, None] * frequency[None, :]
    cosine = jnp.cos(angle)
    sine_part = jnp.sin(angle)
    lower_half = values[..., :half_width]
    upper_half = values[..., half_width:]
    return jnp.concatenate(
        [
            lower_half * cosine - upper_half * sine_part,
            lower_half * sine_part + upper_half * cosine,
        ],
        axis=-1,
    )


LANES = 128


def packed(x):
    rows, width = x.shape[-2:]
    if (rows * width) % LANES:
        return x
    return x.reshape(x.shape[:-2] + (rows * width // LANES, LANES))


def unpacked(x, rows, width):
    return x.reshape(x.shape[:-2] + (rows, width))


def gathered_packed(x, axis_name):
    rows, width = x.shape[-2:]
    return unpacked(gathered(packed(x), axis_name), rows, width)


def head_attention(hidden_all, norm_gain, qkv_weight, positions):
    group = hidden_all.shape[0]
    attn_width = norm_gain.shape[0]
    squares = jnp.sum(hidden_all * hidden_all, axis=(0, 3))
    gain_blocks = norm_gain.reshape(group, 1, 1, attn_width // group)
    qkv_blocks = qkv_weight.reshape(group, attn_width // group, qkv_weight.shape[1])
    projected = jnp.einsum(
        "nbtj,njo->bto", hidden_all * gain_blocks, qkv_blocks, precision=MATMUL_PRECISION
    )
    root_mean = jnp.sqrt(squares / attn_width + 1e-06)
    projected = projected / root_mean[..., None]
    head_extent = qkv_weight.shape[1] // 3
    query_rows = rotate(projected[..., :head_extent], positions) / math.sqrt(head_extent)
    key_matrix = rotate(projected[..., head_extent : 2 * head_extent], positions)
    return query_rows, key_matrix, projected[..., 2 * head_extent :]


def attention_by_batch(pooled, up_weight, norm_gain, qkv_weight, out_weight):
    batch_count, pooled_rows, channels = pooled.shape
    seq = lax.axis_size("seq")
    group = lax.axis_size(CHANNELS)
    per = batch_count // seq
    length = seq * pooled_rows
    mine = lax.all_to_all(pooled.reshape(seq, per, pooled_rows, channels), "seq", 0, 0, tiled=True)
    mine = jnp.transpose(mine, (1, 0, 2, 3)).reshape(per, length, channels)
    pooled_all = gathered_packed(mine, CHANNELS)
    up_blocks = up_weight.reshape(up_weight.shape[0], group, channels)
    hidden = jnp.einsum("nbti,oni->bto", pooled_all, up_blocks, precision=MATMUL_PRECISION)
    hidden_all = gathered_packed(hidden, CHANNELS)
    positions = jnp.arange(length, dtype=jnp.int32).astype(jnp.float32)
    query_rows, key_matrix, value_matrix = head_attention(hidden_all, norm_gain, qkv_weight, positions)
    attention_scores = jnp.einsum(
        "btc,bxc->btx", query_rows, key_matrix, precision=MATMUL_PRECISION
    )
    top = jnp.max(attention_scores, axis=2)
    probabilities = jnp.exp(attention_scores - top[..., None])
    denominator = jnp.sum(probabilities, axis=2)
    weighted_values = jnp.einsum(
        "btx,bxe->bte", probabilities, value_matrix, precision=MATMUL_PRECISION
    )
    head_result = weighted_values / denominator[..., None]
    out_width = out_weight.shape[1] // group
    out_blocks = out_weight.reshape(out_weight.shape[0], group, out_width)
    shares = jnp.einsum("btd,dne->nbte", head_result, out_blocks, precision=MATMUL_PRECISION)
    summed = jnp.sum(lax.all_to_all(packed(shares), CHANNELS, 0, 0, tiled=True), axis=0)
    summed = unpacked(summed, length, out_width)
    by_block = jnp.transpose(summed.reshape(per, seq, pooled_rows, out_width), (1, 0, 2, 3))
    back = lax.all_to_all(packed(by_block), "seq", 0, 0, tiled=True)
    return unpacked(back, pooled_rows, out_width).reshape(batch_count, pooled_rows, out_width)


def attention_by_position(pooled, up_weight, norm_gain, qkv_weight, out_weight):
    batch_count, pooled_rows, channels = pooled.shape
    group = lax.axis_size(CHANNELS)
    pooled_all = gathered_packed(pooled, CHANNELS)
    up_blocks = up_weight.reshape(up_weight.shape[0], group, channels)
    hidden = jnp.einsum("nbti,oni->bto", pooled_all, up_blocks, precision=MATMUL_PRECISION)
    hidden_all = gathered_packed(hidden, CHANNELS)
    positions = (
        lax.axis_index("seq") * pooled_rows + jnp.arange(pooled_rows, dtype=jnp.int32)
    ).astype(jnp.float32)
    query_rows, key_matrix, value_matrix = head_attention(hidden_all, norm_gain, qkv_weight, positions)
    head_extent = query_rows.shape[-1]
    keys_and_values = jnp.concatenate([key_matrix, value_matrix], axis=2)
    kv_all = gathered(keys_and_values, "seq")
    attention_scores = jnp.einsum(
        "btc,nbxc->btnx", query_rows, kv_all[..., :head_extent], precision=MATMUL_PRECISION
    )
    top = jnp.max(attention_scores, axis=(2, 3))
    probabilities = jnp.exp(attention_scores - top[..., None, None])
    denominator = jnp.sum(probabilities, axis=(2, 3))
    weighted_values = jnp.einsum(
        "btnx,nbxe->bte", probabilities, kv_all[..., head_extent:], precision=MATMUL_PRECISION
    )
    head_result = weighted_values / denominator[..., None]
    out_width = out_weight.shape[1] // group
    out_blocks = out_weight.reshape(out_weight.shape[0], group, out_width)
    shares = jnp.einsum("btd,dne->nbte", head_result, out_blocks, precision=MATMUL_PRECISION)
    summed = jnp.sum(lax.all_to_all(packed(shares), CHANNELS, 0, 0, tiled=True), axis=0)
    return unpacked(summed, pooled_rows, out_width)


def per_device(
    features,
    first_channel_scale,
    first_channel_shift,
    first_conv_bias,
    first_kernel_taps,
    second_channel_scale,
    second_channel_shift,
    second_conv_bias,
    second_kernel_taps,
    up_weight,
    norm_gain,
    qkv_weight,
    out_weight,
):
    batch_count = features.shape[0]
    channels = features.shape[1]
    row_count = features.shape[2]
    first_part = convolution_block(
        features,
        first_channel_scale,
        first_channel_shift,
        first_conv_bias,
        first_kernel_taps,
        FIRST_DILATION,
    )
    tower_skip_output = convolution_block(
        first_part,
        second_channel_scale,
        second_channel_shift,
        second_conv_bias,
        second_kernel_taps,
        SECOND_DILATION,
    )
    pooled_rows = row_count // POOL
    pooled = jnp.transpose(
        jnp.max(tower_skip_output.reshape(batch_count, channels, pooled_rows, POOL), axis=3),
        (0, 2, 1),
    )
    if batch_count % lax.axis_size("seq") == 0:
        attended = attention_by_batch(pooled, up_weight, norm_gain, qkv_weight, out_weight)
    else:
        attended = attention_by_position(pooled, up_weight, norm_gain, qkv_weight, out_weight)
    return (tower_skip_output, attended)


def solution(mesh):
    placed = (
        P(None, CHANNELS, "seq"),
        P(CHANNELS),
        P(CHANNELS),
        P(CHANNELS),
        P(None, CHANNELS, None),
        P(CHANNELS),
        P(CHANNELS),
        P(CHANNELS),
        P(None, CHANNELS, None),
        P(CHANNELS, None),
        P(),
        P(None, CHANNELS),
        P(CHANNELS, None),
    )
    return jax.shard_map(
        per_device,
        mesh=mesh,
        in_specs=placed,
        out_specs=(P(None, CHANNELS, "seq"), P(None, "seq", CHANNELS)),
        check_vma=False,
    )
```

```python
import math

import jax
import jax.numpy as jnp
from jax import lax
from jax.sharding import PartitionSpec as P

FIRST_DILATION = 2
SECOND_DILATION = 4
POOL = 8
TAPS = 5

MATMUL_PRECISION = lax.Precision.HIGH
CHANNELS = ("crow", "ccol")


def gathered(x, axis_name):
    count = lax.axis_size(axis_name)
    copies = jnp.broadcast_to(x[None], (count,) + x.shape)
    return lax.all_to_all(copies, axis_name, 0, 0, tiled=True)


def summed_scatter(x, axis_name):
    return jnp.sum(lax.all_to_all(x, axis_name, 0, 0, tiled=True), axis=0)


def swap_ccol(x):
    return lax.ppermute(x, "ccol", [(0, 1), (1, 0)])


def shifted_in(edge, forward):
    count = lax.axis_size("seq")
    if forward:
        pairs = [(i, i + 1) for i in range(count - 1)]
    else:
        pairs = [(i + 1, i) for i in range(count - 1)]
    return lax.ppermute(edge, "seq", pairs)


def activation(inputs, bn_scale, bn_shift):
    return jax.nn.gelu(inputs * bn_scale[:, None] + bn_shift[:, None], approximate=False)


def partner(index, step, count):
    if count & (count - 1) == 0:
        return index ^ step
    return (index + step) % count


def channel_blocks(activated):
    by_row = gathered(activated, "crow")
    return by_row, swap_ccol(by_row)


def convolution_rest(inputs, blocks, conv_bias, kernel, dilation):
    by_row, other_core = blocks
    core = lax.axis_index("ccol")
    tap_count, out_count, in_count = kernel.shape
    row_count = lax.axis_size("crow")
    block = in_count // (2 * row_count)
    weights = jnp.transpose(kernel.reshape(tap_count * out_count, in_count))
    weights = weights.reshape(row_count, 2, block, tap_count * out_count)
    own_weights = lax.dynamic_index_in_dim(weights, core, axis=1, keepdims=False)
    other_weights = lax.dynamic_index_in_dim(weights, 1 - core, axis=1, keepdims=False)
    products = jnp.einsum(
        "rbit,rio->bot", by_row, own_weights, precision=MATMUL_PRECISION
    ) + jnp.einsum("rbit,rio->bot", other_core, other_weights, precision=MATMUL_PRECISION)
    batch_count, rows = inputs.shape[0], inputs.shape[2]
    products = products.reshape(batch_count, tap_count, out_count, rows)
    width = 2 * dilation
    padded = jnp.pad(products, ((0, 0), (0, 0), (0, 0), (2 * width, 2 * width)))
    spread = None
    for tap_index in range(tap_count):
        offset = tap_index * dilation
        term = padded[:, tap_index, :, offset : offset + rows + 2 * width]
        spread = term if spread is None else spread + term
    to_left = jnp.swapaxes(spread[..., :width], 1, 2)
    to_right = jnp.swapaxes(spread[..., rows + width :], 1, 2)
    from_left = jnp.swapaxes(shifted_in(to_right, True), 1, 2)
    from_right = jnp.swapaxes(shifted_in(to_left, False), 1, 2)
    edges = jnp.concatenate(
        [from_left, jnp.zeros((batch_count, out_count, rows - 2 * width), jnp.float32), from_right],
        axis=2,
    )
    summed = spread[..., width : width + rows] + edges
    return inputs + summed + conv_bias[:, None]


def tower(features, first_layer, second_layer, halves):
    piece = features.shape[0] // halves
    parts = [features[h * piece : (h + 1) * piece] for h in range(halves)]
    stages = []
    for layer_index, layer in enumerate((first_layer, second_layer)):
        bn_scale, bn_shift, conv_bias, kernel, dilation = layer
        stages.append(layer)
    previous = None
    inputs = list(parts)
    outputs = [None] * halves
    pending = {}
    sequence = [(layer_index, h) for layer_index in range(2) for h in range(halves)]
    done_blocks = {}
    for position, (layer_index, h) in enumerate(sequence):
        bn_scale, bn_shift, conv_bias, kernel, dilation = stages[layer_index]
        if layer_index == 1:
            lower = done_blocks.pop((0, h))
            inputs[h] = convolution_rest(inputs[h], lower, *stages[0][2:])
        activated = activation(inputs[h], bn_scale, bn_shift)
        if previous is not None:
            done_blocks[last_key] = previous
        blocks = channel_blocks(activated)
        previous = blocks
        last_key = (layer_index, h)
    done_blocks[last_key] = previous
    for h in range(halves):
        outputs[h] = convolution_rest(inputs[h], done_blocks.pop((1, h)), *stages[1][2:])
    return jnp.concatenate(outputs, axis=0)


def rotate(values, positions):
    half_width = values.shape[-1] // 2
    frequency = jnp.exp(
        -math.log(10000.0) * jnp.arange(half_width).astype(jnp.float32) / half_width
    )
    angle = positions[:, None] * frequency[None, :]
    cosine = jnp.cos(angle)
    sine_part = jnp.sin(angle)
    lower_half = values[..., :half_width]
    upper_half = values[..., half_width:]
    return jnp.concatenate(
        [
            lower_half * cosine - upper_half * sine_part,
            lower_half * sine_part + upper_half * cosine,
        ],
        axis=-1,
    )


LANES = 128


def packed(x):
    rows, width = x.shape[-2:]
    if (rows * width) % LANES:
        return x
    return x.reshape(x.shape[:-2] + (rows * width // LANES, LANES))


def unpacked(x, rows, width):
    return x.reshape(x.shape[:-2] + (rows, width))


def gathered_packed(x, axis_name):
    rows, width = x.shape[-2:]
    return unpacked(gathered(packed(x), axis_name), rows, width)


def head_attention(hidden_all, norm_gain, qkv_weight, positions):
    group = hidden_all.shape[0]
    attn_width = norm_gain.shape[0]
    squares = jnp.sum(hidden_all * hidden_all, axis=(0, 3))
    gain_blocks = norm_gain.reshape(group, 1, 1, attn_width // group)
    qkv_blocks = qkv_weight.reshape(group, attn_width // group, qkv_weight.shape[1])
    projected = jnp.einsum(
        "nbtj,njo->bto", hidden_all * gain_blocks, qkv_blocks, precision=MATMUL_PRECISION
    )
    root_mean = jnp.sqrt(squares / attn_width + 1e-06)
    projected = projected / root_mean[..., None]
    head_extent = qkv_weight.shape[1] // 3
    query_rows = rotate(projected[..., :head_extent], positions) / math.sqrt(head_extent)
    key_matrix = rotate(projected[..., head_extent : 2 * head_extent], positions)
    return query_rows, key_matrix, projected[..., 2 * head_extent :]


def attention_by_batch(pooled, up_weight, norm_gain, qkv_weight, out_weight):
    batch_count, pooled_rows, channels = pooled.shape
    seq = lax.axis_size("seq")
    group = lax.axis_size(CHANNELS)
    per = batch_count // seq
    length = seq * pooled_rows
    mine = lax.all_to_all(pooled.reshape(seq, per, pooled_rows, channels), "seq", 0, 0, tiled=True)
    mine = jnp.transpose(mine, (1, 0, 2, 3)).reshape(per, length, channels)
    pooled_all = gathered_packed(mine, CHANNELS)
    up_blocks = up_weight.reshape(up_weight.shape[0], group, channels)
    hidden = jnp.einsum("nbti,oni->bto", pooled_all, up_blocks, precision=MATMUL_PRECISION)
    hidden_all = gathered_packed(hidden, CHANNELS)
    positions = jnp.arange(length, dtype=jnp.int32).astype(jnp.float32)
    query_rows, key_matrix, value_matrix = head_attention(hidden_all, norm_gain, qkv_weight, positions)
    attention_scores = jnp.einsum(
        "btc,bxc->btx", query_rows, key_matrix, precision=MATMUL_PRECISION
    )
    top = jnp.max(attention_scores, axis=2)
    probabilities = jnp.exp(attention_scores - top[..., None])
    denominator = jnp.sum(probabilities, axis=2)
    weighted_values = jnp.einsum(
        "btx,bxe->bte", probabilities, value_matrix, precision=MATMUL_PRECISION
    )
    head_result = weighted_values / denominator[..., None]
    out_width = out_weight.shape[1] // group
    out_blocks = out_weight.reshape(out_weight.shape[0], group, out_width)
    shares = jnp.einsum("btd,dne->nbte", head_result, out_blocks, precision=MATMUL_PRECISION)
    summed = jnp.sum(lax.all_to_all(packed(shares), CHANNELS, 0, 0, tiled=True), axis=0)
    summed = unpacked(summed, length, out_width)
    by_block = jnp.transpose(summed.reshape(per, seq, pooled_rows, out_width), (1, 0, 2, 3))
    back = lax.all_to_all(packed(by_block), "seq", 0, 0, tiled=True)
    return unpacked(back, pooled_rows, out_width).reshape(batch_count, pooled_rows, out_width)


def attention_by_position(pooled, up_weight, norm_gain, qkv_weight, out_weight):
    batch_count, pooled_rows, channels = pooled.shape
    group = lax.axis_size(CHANNELS)
    pooled_all = gathered_packed(pooled, CHANNELS)
    up_blocks = up_weight.reshape(up_weight.shape[0], group, channels)
    hidden = jnp.einsum("nbti,oni->bto", pooled_all, up_blocks, precision=MATMUL_PRECISION)
    hidden_all = gathered_packed(hidden, CHANNELS)
    positions = (
        lax.axis_index("seq") * pooled_rows + jnp.arange(pooled_rows, dtype=jnp.int32)
    ).astype(jnp.float32)
    query_rows, key_matrix, value_matrix = head_attention(hidden_all, norm_gain, qkv_weight, positions)
    head_extent = query_rows.shape[-1]
    keys_and_values = jnp.concatenate([key_matrix, value_matrix], axis=2)
    kv_all = gathered(keys_and_values, "seq")
    attention_scores = jnp.einsum(
        "btc,nbxc->btnx", query_rows, kv_all[..., :head_extent], precision=MATMUL_PRECISION
    )
    top = jnp.max(attention_scores, axis=(2, 3))
    probabilities = jnp.exp(attention_scores - top[..., None, None])
    denominator = jnp.sum(probabilities, axis=(2, 3))
    weighted_values = jnp.einsum(
        "btnx,nbxe->bte", probabilities, kv_all[..., head_extent:], precision=MATMUL_PRECISION
    )
    head_result = weighted_values / denominator[..., None]
    out_width = out_weight.shape[1] // group
    out_blocks = out_weight.reshape(out_weight.shape[0], group, out_width)
    shares = jnp.einsum("btd,dne->nbte", head_result, out_blocks, precision=MATMUL_PRECISION)
    summed = jnp.sum(lax.all_to_all(packed(shares), CHANNELS, 0, 0, tiled=True), axis=0)
    return unpacked(summed, pooled_rows, out_width)


def per_device(
    features,
    first_channel_scale,
    first_channel_shift,
    first_conv_bias,
    first_kernel_taps,
    second_channel_scale,
    second_channel_shift,
    second_conv_bias,
    second_kernel_taps,
    up_weight,
    norm_gain,
    qkv_weight,
    out_weight,
):
    batch_count = features.shape[0]
    channels = features.shape[1]
    row_count = features.shape[2]
    halves = 2 if batch_count % 2 == 0 else 1
    tower_skip_output = tower(
        features,
        (first_channel_scale, first_channel_shift, first_conv_bias, first_kernel_taps, FIRST_DILATION),
        (second_channel_scale, second_channel_shift, second_conv_bias, second_kernel_taps, SECOND_DILATION),
        halves,
    )
    pooled_rows = row_count // POOL
    pooled = jnp.transpose(
        jnp.max(tower_skip_output.reshape(batch_count, channels, pooled_rows, POOL), axis=3),
        (0, 2, 1),
    )
    if batch_count % lax.axis_size("seq") == 0:
        attended = attention_by_batch(pooled, up_weight, norm_gain, qkv_weight, out_weight)
    else:
        attended = attention_by_position(pooled, up_weight, norm_gain, qkv_weight, out_weight)
    return (tower_skip_output, attended)


def solution(mesh):
    placed = (
        P(None, CHANNELS, "seq"),
        P(CHANNELS),
        P(CHANNELS),
        P(CHANNELS),
        P(None, CHANNELS, None),
        P(CHANNELS),
        P(CHANNELS),
        P(CHANNELS),
        P(None, CHANNELS, None),
        P(CHANNELS, None),
        P(),
        P(None, CHANNELS),
        P(CHANNELS, None),
    )
    return jax.shard_map(
        per_device,
        mesh=mesh,
        in_specs=placed,
        out_specs=(P(None, CHANNELS, "seq"), P(None, "seq", CHANNELS)),
        check_vma=False,
    )
```

```python
import math

import jax
import jax.numpy as jnp
from jax import lax
from jax.sharding import PartitionSpec as P

FIRST_DILATION = 2
SECOND_DILATION = 4
POOL = 8
TAPS = 5

MATMUL_PRECISION = lax.Precision.HIGH
CHANNELS = ("crow", "ccol")


def gathered(x, axis_name):
    count = lax.axis_size(axis_name)
    copies = jnp.broadcast_to(x[None], (count,) + x.shape)
    return lax.all_to_all(copies, axis_name, 0, 0, tiled=True)


def summed_scatter(x, axis_name):
    return jnp.sum(lax.all_to_all(x, axis_name, 0, 0, tiled=True), axis=0)


def swap_ccol(x):
    return lax.ppermute(x, "ccol", [(0, 1), (1, 0)])


def shifted_in(edge, forward):
    count = lax.axis_size("seq")
    if forward:
        pairs = [(i, i + 1) for i in range(count - 1)]
    else:
        pairs = [(i + 1, i) for i in range(count - 1)]
    return lax.ppermute(edge, "seq", pairs)


def convolution_block(inputs, bn_scale, bn_shift, conv_bias, kernel, dilation):
    activated = jax.nn.gelu(inputs * bn_scale[:, None] + bn_shift[:, None], approximate=False)
    by_row = gathered(activated, "crow")
    other_core = swap_ccol(by_row)
    core = lax.axis_index("ccol")
    tap_count, out_count, in_count = kernel.shape
    row_count = lax.axis_size("crow")
    block = in_count // (2 * row_count)
    weights = jnp.transpose(kernel, (2, 0, 1)).reshape(row_count, 2, block, tap_count, out_count)
    own_weights = lax.dynamic_index_in_dim(weights, core, axis=1, keepdims=False)
    other_weights = lax.dynamic_index_in_dim(weights, 1 - core, axis=1, keepdims=False)
    products = jnp.einsum(
        "rbit,rikp->kbtp", by_row, own_weights, precision=MATMUL_PRECISION
    ) + jnp.einsum("rbit,rikp->kbtp", other_core, other_weights, precision=MATMUL_PRECISION)
    batch_count, rows = inputs.shape[0], inputs.shape[2]
    width = 2 * dilation
    padded = jnp.pad(products, ((0, 0), (0, 0), (2 * width, 2 * width), (0, 0)))
    spread = None
    for tap_index in range(tap_count):
        offset = tap_index * dilation
        term = padded[tap_index, :, offset : offset + rows + 2 * width, :]
        spread = term if spread is None else spread + term
    spread = jnp.swapaxes(spread, 1, 2)
    to_left = jnp.swapaxes(spread[..., :width], 1, 2)
    to_right = jnp.swapaxes(spread[..., rows + width :], 1, 2)
    from_left = jnp.swapaxes(shifted_in(to_right, True), 1, 2)
    from_right = jnp.swapaxes(shifted_in(to_left, False), 1, 2)
    edges = jnp.concatenate(
        [from_left, jnp.zeros((batch_count, out_count, rows - 2 * width), jnp.float32), from_right],
        axis=2,
    )
    summed = spread[..., width : width + rows] + edges
    return inputs + summed + conv_bias[:, None]


def rotate(values, positions):
    half_width = values.shape[-1] // 2
    frequency = jnp.exp(
        -math.log(10000.0) * jnp.arange(half_width).astype(jnp.float32) / half_width
    )
    angle = positions[:, None] * frequency[None, :]
    cosine = jnp.cos(angle)
    sine_part = jnp.sin(angle)
    lower_half = values[..., :half_width]
    upper_half = values[..., half_width:]
    return jnp.concatenate(
        [
            lower_half * cosine - upper_half * sine_part,
            lower_half * sine_part + upper_half * cosine,
        ],
        axis=-1,
    )


LANES = 128


def packed(x):
    rows, width = x.shape[-2:]
    if (rows * width) % LANES:
        return x
    return x.reshape(x.shape[:-2] + (rows * width // LANES, LANES))


def unpacked(x, rows, width):
    return x.reshape(x.shape[:-2] + (rows, width))


def gathered_packed(x, axis_name):
    rows, width = x.shape[-2:]
    return unpacked(gathered(packed(x), axis_name), rows, width)


def head_attention(hidden_all, norm_gain, qkv_weight, positions):
    group = hidden_all.shape[0]
    attn_width = norm_gain.shape[0]
    squares = jnp.sum(hidden_all * hidden_all, axis=(0, 3))
    gain_blocks = norm_gain.reshape(group, 1, 1, attn_width // group)
    qkv_blocks = qkv_weight.reshape(group, attn_width // group, qkv_weight.shape[1])
    projected = jnp.einsum(
        "nbtj,njo->bto", hidden_all * gain_blocks, qkv_blocks, precision=MATMUL_PRECISION
    )
    root_mean = jnp.sqrt(squares / attn_width + 1e-06)
    projected = projected / root_mean[..., None]
    head_extent = qkv_weight.shape[1] // 3
    query_rows = rotate(projected[..., :head_extent], positions) / math.sqrt(head_extent)
    key_matrix = rotate(projected[..., head_extent : 2 * head_extent], positions)
    return query_rows, key_matrix, projected[..., 2 * head_extent :]


def attention_by_batch(pooled, up_weight, norm_gain, qkv_weight, out_weight):
    batch_count, pooled_rows, channels = pooled.shape
    seq = lax.axis_size("seq")
    group = lax.axis_size(CHANNELS)
    per = batch_count // seq
    length = seq * pooled_rows
    mine = lax.all_to_all(pooled.reshape(seq, per, pooled_rows, channels), "seq", 0, 0, tiled=True)
    mine = jnp.transpose(mine, (1, 0, 2, 3)).reshape(per, length, channels)
    pooled_all = gathered_packed(mine, CHANNELS)
    up_blocks = up_weight.reshape(up_weight.shape[0], group, channels)
    hidden = jnp.einsum("nbti,oni->bto", pooled_all, up_blocks, precision=MATMUL_PRECISION)
    hidden_all = gathered_packed(hidden, CHANNELS)
    positions = jnp.arange(length, dtype=jnp.int32).astype(jnp.float32)
    query_rows, key_matrix, value_matrix = head_attention(hidden_all, norm_gain, qkv_weight, positions)
    attention_scores = jnp.einsum(
        "btc,bxc->btx", query_rows, key_matrix, precision=MATMUL_PRECISION
    )
    top = jnp.max(attention_scores, axis=2)
    probabilities = jnp.exp(attention_scores - top[..., None])
    denominator = jnp.sum(probabilities, axis=2)
    weighted_values = jnp.einsum(
        "btx,bxe->bte", probabilities, value_matrix, precision=MATMUL_PRECISION
    )
    head_result = weighted_values / denominator[..., None]
    out_width = out_weight.shape[1] // group
    out_blocks = out_weight.reshape(out_weight.shape[0], group, out_width)
    shares = jnp.einsum("btd,dne->nbte", head_result, out_blocks, precision=MATMUL_PRECISION)
    summed = jnp.sum(lax.all_to_all(packed(shares), CHANNELS, 0, 0, tiled=True), axis=0)
    summed = unpacked(summed, length, out_width)
    by_block = jnp.transpose(summed.reshape(per, seq, pooled_rows, out_width), (1, 0, 2, 3))
    back = lax.all_to_all(packed(by_block), "seq", 0, 0, tiled=True)
    return unpacked(back, pooled_rows, out_width).reshape(batch_count, pooled_rows, out_width)


def attention_by_position(pooled, up_weight, norm_gain, qkv_weight, out_weight):
    batch_count, pooled_rows, channels = pooled.shape
    group = lax.axis_size(CHANNELS)
    pooled_all = gathered_packed(pooled, CHANNELS)
    up_blocks = up_weight.reshape(up_weight.shape[0], group, channels)
    hidden = jnp.einsum("nbti,oni->bto", pooled_all, up_blocks, precision=MATMUL_PRECISION)
    hidden_all = gathered_packed(hidden, CHANNELS)
    positions = (
        lax.axis_index("seq") * pooled_rows + jnp.arange(pooled_rows, dtype=jnp.int32)
    ).astype(jnp.float32)
    query_rows, key_matrix, value_matrix = head_attention(hidden_all, norm_gain, qkv_weight, positions)
    head_extent = query_rows.shape[-1]
    keys_and_values = jnp.concatenate([key_matrix, value_matrix], axis=2)
    kv_all = gathered(keys_and_values, "seq")
    attention_scores = jnp.einsum(
        "btc,nbxc->btnx", query_rows, kv_all[..., :head_extent], precision=MATMUL_PRECISION
    )
    top = jnp.max(attention_scores, axis=(2, 3))
    probabilities = jnp.exp(attention_scores - top[..., None, None])
    denominator = jnp.sum(probabilities, axis=(2, 3))
    weighted_values = jnp.einsum(
        "btnx,nbxe->bte", probabilities, kv_all[..., head_extent:], precision=MATMUL_PRECISION
    )
    head_result = weighted_values / denominator[..., None]
    out_width = out_weight.shape[1] // group
    out_blocks = out_weight.reshape(out_weight.shape[0], group, out_width)
    shares = jnp.einsum("btd,dne->nbte", head_result, out_blocks, precision=MATMUL_PRECISION)
    summed = jnp.sum(lax.all_to_all(packed(shares), CHANNELS, 0, 0, tiled=True), axis=0)
    return unpacked(summed, pooled_rows, out_width)


def per_device(
    features,
    first_channel_scale,
    first_channel_shift,
    first_conv_bias,
    first_kernel_taps,
    second_channel_scale,
    second_channel_shift,
    second_conv_bias,
    second_kernel_taps,
    up_weight,
    norm_gain,
    qkv_weight,
    out_weight,
):
    batch_count = features.shape[0]
    channels = features.shape[1]
    row_count = features.shape[2]
    first_part = convolution_block(
        features,
        first_channel_scale,
        first_channel_shift,
        first_conv_bias,
        first_kernel_taps,
        FIRST_DILATION,
    )
    tower_skip_output = convolution_block(
        first_part,
        second_channel_scale,
        second_channel_shift,
        second_conv_bias,
        second_kernel_taps,
        SECOND_DILATION,
    )
    pooled_rows = row_count // POOL
    pooled = jnp.transpose(
        jnp.max(tower_skip_output.reshape(batch_count, channels, pooled_rows, POOL), axis=3),
        (0, 2, 1),
    )
    if batch_count % lax.axis_size("seq") == 0:
        attended = attention_by_batch(pooled, up_weight, norm_gain, qkv_weight, out_weight)
    else:
        attended = attention_by_position(pooled, up_weight, norm_gain, qkv_weight, out_weight)
    return (tower_skip_output, attended)


def solution(mesh):
    placed = (
        P(None, CHANNELS, "seq"),
        P(CHANNELS),
        P(CHANNELS),
        P(CHANNELS),
        P(None, CHANNELS, None),
        P(CHANNELS),
        P(CHANNELS),
        P(CHANNELS),
        P(None, CHANNELS, None),
        P(CHANNELS, None),
        P(),
        P(None, CHANNELS),
        P(CHANNELS, None),
    )
    return jax.shard_map(
        per_device,
        mesh=mesh,
        in_specs=placed,
        out_specs=(P(None, CHANNELS, "seq"), P(None, "seq", CHANNELS)),
        check_vma=False,
    )
```

```python
import math

import jax
import jax.numpy as jnp
from jax import lax
from jax.sharding import PartitionSpec as P

FIRST_DILATION = 2
SECOND_DILATION = 4
POOL = 8
TAPS = 5

MATMUL_PRECISION = lax.Precision.HIGH
CHANNELS = ("crow", "ccol")


def gathered(x, axis_name):
    count = lax.axis_size(axis_name)
    copies = jnp.broadcast_to(x[None], (count,) + x.shape)
    return lax.all_to_all(copies, axis_name, 0, 0, tiled=True)


def summed_scatter(x, axis_name):
    return jnp.sum(lax.all_to_all(x, axis_name, 0, 0, tiled=True), axis=0)


def swap_ccol(x):
    return lax.ppermute(x, "ccol", [(0, 1), (1, 0)])


def shifted_in(edge, forward):
    count = lax.axis_size("seq")
    if forward:
        pairs = [(i, i + 1) for i in range(count - 1)]
    else:
        pairs = [(i + 1, i) for i in range(count - 1)]
    return lax.ppermute(edge, "seq", pairs)


def convolution_block(inputs, bn_scale, bn_shift, conv_bias, kernel, dilation):
    activated = jax.nn.gelu(inputs * bn_scale[:, None] + bn_shift[:, None], approximate=False)
    by_row = gathered(activated, "crow")
    other_core = swap_ccol(by_row)
    core = lax.axis_index("ccol")
    tap_count, out_count, in_count = kernel.shape
    row_count, batch_count, block, rows = by_row.shape
    slot = lax.broadcasted_iota(jnp.int32, (1, 2, 1, 1, 1), 1)
    ordered = jnp.where(slot == core, by_row[:, None], other_core[:, None])
    ordered = jnp.transpose(ordered, (2, 4, 0, 1, 3)).reshape(batch_count, rows, in_count)
    products = jnp.einsum("btc,koc->kbto", ordered, kernel, precision=MATMUL_PRECISION)
    batch_count, rows = inputs.shape[0], inputs.shape[2]
    width = 2 * dilation
    padded = jnp.pad(products, ((0, 0), (0, 0), (2 * width, 2 * width), (0, 0)))
    spread = None
    for tap_index in range(tap_count):
        offset = tap_index * dilation
        term = padded[tap_index, :, offset : offset + rows + 2 * width, :]
        spread = term if spread is None else spread + term
    spread = jnp.swapaxes(spread, 1, 2)
    to_left = jnp.swapaxes(spread[..., :width], 1, 2)
    to_right = jnp.swapaxes(spread[..., rows + width :], 1, 2)
    from_left = jnp.swapaxes(shifted_in(to_right, True), 1, 2)
    from_right = jnp.swapaxes(shifted_in(to_left, False), 1, 2)
    edges = jnp.concatenate(
        [from_left, jnp.zeros((batch_count, out_count, rows - 2 * width), jnp.float32), from_right],
        axis=2,
    )
    summed = spread[..., width : width + rows] + edges
    return inputs + summed + conv_bias[:, None]


def rotate(values, positions):
    half_width = values.shape[-1] // 2
    frequency = jnp.exp(
        -math.log(10000.0) * jnp.arange(half_width).astype(jnp.float32) / half_width
    )
    angle = positions[:, None] * frequency[None, :]
    cosine = jnp.cos(angle)
    sine_part = jnp.sin(angle)
    lower_half = values[..., :half_width]
    upper_half = values[..., half_width:]
    return jnp.concatenate(
        [
            lower_half * cosine - upper_half * sine_part,
            lower_half * sine_part + upper_half * cosine,
        ],
        axis=-1,
    )


LANES = 128


def packed(x):
    rows, width = x.shape[-2:]
    if (rows * width) % LANES:
        return x
    return x.reshape(x.shape[:-2] + (rows * width // LANES, LANES))


def unpacked(x, rows, width):
    return x.reshape(x.shape[:-2] + (rows, width))


def gathered_packed(x, axis_name):
    rows, width = x.shape[-2:]
    return unpacked(gathered(packed(x), axis_name), rows, width)


def head_attention(hidden_all, norm_gain, qkv_weight, positions):
    group = hidden_all.shape[0]
    attn_width = norm_gain.shape[0]
    squares = jnp.sum(hidden_all * hidden_all, axis=(0, 3))
    gain_blocks = norm_gain.reshape(group, 1, 1, attn_width // group)
    qkv_blocks = qkv_weight.reshape(group, attn_width // group, qkv_weight.shape[1])
    projected = jnp.einsum(
        "nbtj,njo->bto", hidden_all * gain_blocks, qkv_blocks, precision=MATMUL_PRECISION
    )
    root_mean = jnp.sqrt(squares / attn_width + 1e-06)
    projected = projected / root_mean[..., None]
    head_extent = qkv_weight.shape[1] // 3
    query_rows = rotate(projected[..., :head_extent], positions) / math.sqrt(head_extent)
    key_matrix = rotate(projected[..., head_extent : 2 * head_extent], positions)
    return query_rows, key_matrix, projected[..., 2 * head_extent :]


def attention_by_batch(pooled, up_weight, norm_gain, qkv_weight, out_weight):
    batch_count, pooled_rows, channels = pooled.shape
    seq = lax.axis_size("seq")
    group = lax.axis_size(CHANNELS)
    per = batch_count // seq
    length = seq * pooled_rows
    mine = lax.all_to_all(pooled.reshape(seq, per, pooled_rows, channels), "seq", 0, 0, tiled=True)
    mine = jnp.transpose(mine, (1, 0, 2, 3)).reshape(per, length, channels)
    pooled_all = gathered_packed(mine, CHANNELS)
    up_blocks = up_weight.reshape(up_weight.shape[0], group, channels)
    hidden = jnp.einsum("nbti,oni->bto", pooled_all, up_blocks, precision=MATMUL_PRECISION)
    hidden_all = gathered_packed(hidden, CHANNELS)
    positions = jnp.arange(length, dtype=jnp.int32).astype(jnp.float32)
    query_rows, key_matrix, value_matrix = head_attention(hidden_all, norm_gain, qkv_weight, positions)
    attention_scores = jnp.einsum(
        "btc,bxc->btx", query_rows, key_matrix, precision=MATMUL_PRECISION
    )
    top = jnp.max(attention_scores, axis=2)
    probabilities = jnp.exp(attention_scores - top[..., None])
    denominator = jnp.sum(probabilities, axis=2)
    weighted_values = jnp.einsum(
        "btx,bxe->bte", probabilities, value_matrix, precision=MATMUL_PRECISION
    )
    head_result = weighted_values / denominator[..., None]
    out_width = out_weight.shape[1] // group
    out_blocks = out_weight.reshape(out_weight.shape[0], group, out_width)
    shares = jnp.einsum("btd,dne->nbte", head_result, out_blocks, precision=MATMUL_PRECISION)
    summed = jnp.sum(lax.all_to_all(packed(shares), CHANNELS, 0, 0, tiled=True), axis=0)
    summed = unpacked(summed, length, out_width)
    by_block = jnp.transpose(summed.reshape(per, seq, pooled_rows, out_width), (1, 0, 2, 3))
    back = lax.all_to_all(packed(by_block), "seq", 0, 0, tiled=True)
    return unpacked(back, pooled_rows, out_width).reshape(batch_count, pooled_rows, out_width)


def attention_by_position(pooled, up_weight, norm_gain, qkv_weight, out_weight):
    batch_count, pooled_rows, channels = pooled.shape
    group = lax.axis_size(CHANNELS)
    pooled_all = gathered_packed(pooled, CHANNELS)
    up_blocks = up_weight.reshape(up_weight.shape[0], group, channels)
    hidden = jnp.einsum("nbti,oni->bto", pooled_all, up_blocks, precision=MATMUL_PRECISION)
    hidden_all = gathered_packed(hidden, CHANNELS)
    positions = (
        lax.axis_index("seq") * pooled_rows + jnp.arange(pooled_rows, dtype=jnp.int32)
    ).astype(jnp.float32)
    query_rows, key_matrix, value_matrix = head_attention(hidden_all, norm_gain, qkv_weight, positions)
    head_extent = query_rows.shape[-1]
    keys_and_values = jnp.concatenate([key_matrix, value_matrix], axis=2)
    kv_all = gathered(keys_and_values, "seq")
    attention_scores = jnp.einsum(
        "btc,nbxc->btnx", query_rows, kv_all[..., :head_extent], precision=MATMUL_PRECISION
    )
    top = jnp.max(attention_scores, axis=(2, 3))
    probabilities = jnp.exp(attention_scores - top[..., None, None])
    denominator = jnp.sum(probabilities, axis=(2, 3))
    weighted_values = jnp.einsum(
        "btnx,nbxe->bte", probabilities, kv_all[..., head_extent:], precision=MATMUL_PRECISION
    )
    head_result = weighted_values / denominator[..., None]
    out_width = out_weight.shape[1] // group
    out_blocks = out_weight.reshape(out_weight.shape[0], group, out_width)
    shares = jnp.einsum("btd,dne->nbte", head_result, out_blocks, precision=MATMUL_PRECISION)
    summed = jnp.sum(lax.all_to_all(packed(shares), CHANNELS, 0, 0, tiled=True), axis=0)
    return unpacked(summed, pooled_rows, out_width)


def per_device(
    features,
    first_channel_scale,
    first_channel_shift,
    first_conv_bias,
    first_kernel_taps,
    second_channel_scale,
    second_channel_shift,
    second_conv_bias,
    second_kernel_taps,
    up_weight,
    norm_gain,
    qkv_weight,
    out_weight,
):
    batch_count = features.shape[0]
    channels = features.shape[1]
    row_count = features.shape[2]
    first_part = convolution_block(
        features,
        first_channel_scale,
        first_channel_shift,
        first_conv_bias,
        first_kernel_taps,
        FIRST_DILATION,
    )
    tower_skip_output = convolution_block(
        first_part,
        second_channel_scale,
        second_channel_shift,
        second_conv_bias,
        second_kernel_taps,
        SECOND_DILATION,
    )
    pooled_rows = row_count // POOL
    pooled = jnp.transpose(
        jnp.max(tower_skip_output.reshape(batch_count, channels, pooled_rows, POOL), axis=3),
        (0, 2, 1),
    )
    if batch_count % lax.axis_size("seq") == 0:
        attended = attention_by_batch(pooled, up_weight, norm_gain, qkv_weight, out_weight)
    else:
        attended = attention_by_position(pooled, up_weight, norm_gain, qkv_weight, out_weight)
    return (tower_skip_output, attended)


def solution(mesh):
    placed = (
        P(None, CHANNELS, "seq"),
        P(CHANNELS),
        P(CHANNELS),
        P(CHANNELS),
        P(None, CHANNELS, None),
        P(CHANNELS),
        P(CHANNELS),
        P(CHANNELS),
        P(None, CHANNELS, None),
        P(CHANNELS, None),
        P(),
        P(None, CHANNELS),
        P(CHANNELS, None),
    )
    return jax.shard_map(
        per_device,
        mesh=mesh,
        in_specs=placed,
        out_specs=(P(None, CHANNELS, "seq"), P(None, "seq", CHANNELS)),
        check_vma=False,
    )
```

```python
import math

import jax
import jax.numpy as jnp
from jax import lax
from jax.sharding import PartitionSpec as P

FIRST_DILATION = 2
SECOND_DILATION = 4
POOL = 8
TAPS = 5

MATMUL_PRECISION = lax.Precision.HIGH
CHANNELS = ("crow", "ccol")


def gathered(x, axis_name):
    count = lax.axis_size(axis_name)
    copies = jnp.broadcast_to(x[None], (count,) + x.shape)
    return lax.all_to_all(copies, axis_name, 0, 0, tiled=True)


def summed_scatter(x, axis_name):
    return jnp.sum(lax.all_to_all(x, axis_name, 0, 0, tiled=True), axis=0)


def swap_ccol(x):
    return lax.ppermute(x, "ccol", [(0, 1), (1, 0)])


def shifted_in(edge, forward):
    count = lax.axis_size("seq")
    if forward:
        pairs = [(i, i + 1) for i in range(count - 1)]
    else:
        pairs = [(i + 1, i) for i in range(count - 1)]
    return lax.ppermute(edge, "seq", pairs)


def convolution_block(inputs, bn_scale, bn_shift, conv_bias, kernel, dilation):
    activated = jax.nn.gelu(inputs * bn_scale[:, None] + bn_shift[:, None], approximate=False)
    by_row = gathered(activated, "crow")
    other_core = swap_ccol(by_row)
    core = lax.axis_index("ccol")
    tap_count, out_count, in_count = kernel.shape
    row_count, batch_count, block, rows = by_row.shape
    slot = lax.broadcasted_iota(jnp.int32, (1, 2, 1, 1, 1), 1)
    ordered = jnp.where(slot == core, by_row[:, None], other_core[:, None])
    ordered = jnp.transpose(ordered, (2, 4, 0, 1, 3)).reshape(batch_count, rows, in_count)
    products = jnp.einsum("btc,koc->kbto", ordered, kernel, precision=MATMUL_PRECISION)
    batch_count, rows = inputs.shape[0], inputs.shape[2]
    width = 2 * dilation
    padded = jnp.pad(products, ((0, 0), (0, 0), (2 * width, 2 * width), (0, 0)))
    spread = None
    for tap_index in range(tap_count):
        offset = tap_index * dilation
        term = padded[tap_index, :, offset : offset + rows + 2 * width, :]
        spread = term if spread is None else spread + term
    spread = jnp.swapaxes(spread, 1, 2)
    to_left = jnp.swapaxes(spread[..., :width], 1, 2)
    to_right = jnp.swapaxes(spread[..., rows + width :], 1, 2)
    from_left = jnp.swapaxes(shifted_in(to_right, True), 1, 2)
    from_right = jnp.swapaxes(shifted_in(to_left, False), 1, 2)
    edges = jnp.concatenate(
        [from_left, jnp.zeros((batch_count, out_count, rows - 2 * width), jnp.float32), from_right],
        axis=2,
    )
    summed = spread[..., width : width + rows] + edges
    return inputs + summed + conv_bias[:, None]


def rotate(values, positions):
    half_width = values.shape[-1] // 2
    frequency = jnp.exp(
        -math.log(10000.0) * jnp.arange(half_width).astype(jnp.float32) / half_width
    )
    angle = positions[:, None] * frequency[None, :]
    cosine = jnp.cos(angle)
    sine_part = jnp.sin(angle)
    lower_half = values[..., :half_width]
    upper_half = values[..., half_width:]
    return jnp.concatenate(
        [
            lower_half * cosine - upper_half * sine_part,
            lower_half * sine_part + upper_half * cosine,
        ],
        axis=-1,
    )


LANES = 128


def packed(x):
    rows, width = x.shape[-2:]
    if (rows * width) % LANES:
        return x
    return x.reshape(x.shape[:-2] + (rows * width // LANES, LANES))


def unpacked(x, rows, width):
    return x.reshape(x.shape[:-2] + (rows, width))


def gathered_packed(x, axis_name):
    rows, width = x.shape[-2:]
    return unpacked(gathered(packed(x), axis_name), rows, width)


def head_attention(hidden_all, norm_gain, qkv_weight, positions):
    group = hidden_all.shape[0]
    attn_width = norm_gain.shape[0]
    squares = jnp.sum(hidden_all * hidden_all, axis=(0, 3))
    gain_blocks = norm_gain.reshape(group, 1, 1, attn_width // group)
    qkv_blocks = qkv_weight.reshape(group, attn_width // group, qkv_weight.shape[1])
    projected = jnp.einsum(
        "nbtj,njo->bto", hidden_all * gain_blocks, qkv_blocks, precision=MATMUL_PRECISION
    )
    root_mean = jnp.sqrt(squares / attn_width + 1e-06)
    projected = projected / root_mean[..., None]
    head_extent = qkv_weight.shape[1] // 3
    query_rows = rotate(projected[..., :head_extent], positions) / math.sqrt(head_extent)
    key_matrix = rotate(projected[..., head_extent : 2 * head_extent], positions)
    return query_rows, key_matrix, projected[..., 2 * head_extent :]


def attention_by_batch(pooled, up_weight, norm_gain, qkv_weight, out_weight):
    batch_count, pooled_rows, channels = pooled.shape
    seq = lax.axis_size("seq")
    group = lax.axis_size(CHANNELS)
    per = batch_count // seq
    length = seq * pooled_rows
    mine = lax.all_to_all(pooled.reshape(seq, per, pooled_rows, channels), "seq", 0, 0, tiled=True)
    mine = jnp.transpose(mine, (1, 0, 2, 3)).reshape(per, length, channels)
    pooled_all = gathered_packed(mine, CHANNELS)
    up_blocks = up_weight.reshape(up_weight.shape[0], group, channels)
    hidden = jnp.einsum("nbti,oni->bto", pooled_all, up_blocks, precision=MATMUL_PRECISION)
    hidden_all = gathered_packed(hidden, CHANNELS)
    positions = jnp.arange(length, dtype=jnp.int32).astype(jnp.float32)
    query_rows, key_matrix, value_matrix = head_attention(hidden_all, norm_gain, qkv_weight, positions)
    attention_scores = jnp.einsum(
        "btc,bxc->btx", query_rows, key_matrix, precision=MATMUL_PRECISION
    )
    top = jnp.max(attention_scores, axis=2)
    probabilities = jnp.exp(attention_scores - top[..., None])
    denominator = jnp.sum(probabilities, axis=2)
    weighted_values = jnp.einsum(
        "btx,bxe->bte", probabilities, value_matrix, precision=MATMUL_PRECISION
    )
    head_result = weighted_values / denominator[..., None]
    out_width = out_weight.shape[1] // group
    out_blocks = out_weight.reshape(out_weight.shape[0], group, out_width)
    shares = jnp.einsum("btd,dne->nbte", head_result, out_blocks, precision=MATMUL_PRECISION)
    summed = jnp.sum(lax.all_to_all(shares, CHANNELS, 0, 0, tiled=True), axis=0)
    by_block = jnp.transpose(summed.reshape(per, seq, pooled_rows, out_width), (1, 0, 2, 3))
    back = lax.all_to_all(packed(by_block), "seq", 0, 0, tiled=True)
    return unpacked(back, pooled_rows, out_width).reshape(batch_count, pooled_rows, out_width)


def attention_by_position(pooled, up_weight, norm_gain, qkv_weight, out_weight):
    batch_count, pooled_rows, channels = pooled.shape
    group = lax.axis_size(CHANNELS)
    pooled_all = gathered_packed(pooled, CHANNELS)
    up_blocks = up_weight.reshape(up_weight.shape[0], group, channels)
    hidden = jnp.einsum("nbti,oni->bto", pooled_all, up_blocks, precision=MATMUL_PRECISION)
    hidden_all = gathered_packed(hidden, CHANNELS)
    positions = (
        lax.axis_index("seq") * pooled_rows + jnp.arange(pooled_rows, dtype=jnp.int32)
    ).astype(jnp.float32)
    query_rows, key_matrix, value_matrix = head_attention(hidden_all, norm_gain, qkv_weight, positions)
    head_extent = query_rows.shape[-1]
    keys_and_values = jnp.concatenate([key_matrix, value_matrix], axis=2)
    kv_all = gathered(keys_and_values, "seq")
    attention_scores = jnp.einsum(
        "btc,nbxc->btnx", query_rows, kv_all[..., :head_extent], precision=MATMUL_PRECISION
    )
    top = jnp.max(attention_scores, axis=(2, 3))
    probabilities = jnp.exp(attention_scores - top[..., None, None])
    denominator = jnp.sum(probabilities, axis=(2, 3))
    weighted_values = jnp.einsum(
        "btnx,nbxe->bte", probabilities, kv_all[..., head_extent:], precision=MATMUL_PRECISION
    )
    head_result = weighted_values / denominator[..., None]
    out_width = out_weight.shape[1] // group
    out_blocks = out_weight.reshape(out_weight.shape[0], group, out_width)
    shares = jnp.einsum("btd,dne->nbte", head_result, out_blocks, precision=MATMUL_PRECISION)
    summed = jnp.sum(lax.all_to_all(packed(shares), CHANNELS, 0, 0, tiled=True), axis=0)
    return unpacked(summed, pooled_rows, out_width)


def per_device(
    features,
    first_channel_scale,
    first_channel_shift,
    first_conv_bias,
    first_kernel_taps,
    second_channel_scale,
    second_channel_shift,
    second_conv_bias,
    second_kernel_taps,
    up_weight,
    norm_gain,
    qkv_weight,
    out_weight,
):
    batch_count = features.shape[0]
    channels = features.shape[1]
    row_count = features.shape[2]
    first_part = convolution_block(
        features,
        first_channel_scale,
        first_channel_shift,
        first_conv_bias,
        first_kernel_taps,
        FIRST_DILATION,
    )
    tower_skip_output = convolution_block(
        first_part,
        second_channel_scale,
        second_channel_shift,
        second_conv_bias,
        second_kernel_taps,
        SECOND_DILATION,
    )
    pooled_rows = row_count // POOL
    pooled = jnp.transpose(
        jnp.max(tower_skip_output.reshape(batch_count, channels, pooled_rows, POOL), axis=3),
        (0, 2, 1),
    )
    if batch_count % lax.axis_size("seq") == 0:
        attended = attention_by_batch(pooled, up_weight, norm_gain, qkv_weight, out_weight)
    else:
        attended = attention_by_position(pooled, up_weight, norm_gain, qkv_weight, out_weight)
    return (tower_skip_output, attended)


def solution(mesh):
    placed = (
        P(None, CHANNELS, "seq"),
        P(CHANNELS),
        P(CHANNELS),
        P(CHANNELS),
        P(None, CHANNELS, None),
        P(CHANNELS),
        P(CHANNELS),
        P(CHANNELS),
        P(None, CHANNELS, None),
        P(CHANNELS, None),
        P(),
        P(None, CHANNELS),
        P(CHANNELS, None),
    )
    return jax.shard_map(
        per_device,
        mesh=mesh,
        in_specs=placed,
        out_specs=(P(None, CHANNELS, "seq"), P(None, "seq", CHANNELS)),
        check_vma=False,
    )
```

```python
import math

import jax
import jax.numpy as jnp
from jax import lax
from jax.sharding import PartitionSpec as P

FIRST_DILATION = 2
SECOND_DILATION = 4
POOL = 8
TAPS = 5

MATMUL_PRECISION = lax.Precision.HIGH
CHANNELS = ("crow", "ccol")


def gathered(x, axis_name):
    count = lax.axis_size(axis_name)
    copies = jnp.broadcast_to(x[None], (count,) + x.shape)
    return lax.all_to_all(copies, axis_name, 0, 0, tiled=True)


def summed_scatter(x, axis_name):
    return jnp.sum(lax.all_to_all(x, axis_name, 0, 0, tiled=True), axis=0)


def swap_ccol(x):
    return lax.ppermute(x, "ccol", [(0, 1), (1, 0)])


def shifted_in(edge, forward):
    count = lax.axis_size("seq")
    if forward:
        pairs = [(i, i + 1) for i in range(count - 1)]
    else:
        pairs = [(i + 1, i) for i in range(count - 1)]
    return lax.ppermute(edge, "seq", pairs)


def row_exchange(activated):
    pairs = lambda step: [(j, j ^ step) for j in range(4)]
    across = lax.ppermute(activated, "crow", pairs(1))
    along = lax.ppermute(activated, "crow", pairs(2))
    half = activated.shape[0] // 2
    first = lax.ppermute(across[:half], "crow", pairs(2))
    second = lax.ppermute(along[half:], "crow", pairs(1))
    diagonal = jnp.concatenate([first, second], axis=0)
    return jnp.stack([activated, across, along, diagonal])


def convolution_block(inputs, bn_scale, bn_shift, conv_bias, kernel, dilation):
    activated = jax.nn.gelu(inputs * bn_scale[:, None] + bn_shift[:, None], approximate=False)
    core = lax.axis_index("ccol")
    if lax.axis_size("crow") == 4 and activated.shape[0] % 2 == 0:
        slots = row_exchange(activated)
        other_slots = swap_ccol(slots)
        row = lax.axis_index("crow")
        by_row = jnp.stack([jnp.take(slots, jnp.bitwise_xor(row, r), axis=0) for r in range(4)])
        other_core = jnp.stack([jnp.take(other_slots, jnp.bitwise_xor(row, r), axis=0) for r in range(4)])
    else:
        by_row = gathered(activated, "crow")
        other_core = swap_ccol(by_row)
    tap_count, out_count, in_count = kernel.shape
    row_count, batch_count, block, rows = by_row.shape
    slot = lax.broadcasted_iota(jnp.int32, (1, 2, 1, 1, 1), 1)
    ordered = jnp.where(slot == core, by_row[:, None], other_core[:, None])
    ordered = jnp.transpose(ordered, (2, 4, 0, 1, 3)).reshape(batch_count, rows, in_count)
    products = jnp.einsum("btc,koc->kbto", ordered, kernel, precision=MATMUL_PRECISION)
    batch_count, rows = inputs.shape[0], inputs.shape[2]
    width = 2 * dilation
    padded = jnp.pad(products, ((0, 0), (0, 0), (2 * width, 2 * width), (0, 0)))
    spread = None
    for tap_index in range(tap_count):
        offset = tap_index * dilation
        term = padded[tap_index, :, offset : offset + rows + 2 * width, :]
        spread = term if spread is None else spread + term
    spread = jnp.swapaxes(spread, 1, 2)
    to_left = jnp.swapaxes(spread[..., :width], 1, 2)
    to_right = jnp.swapaxes(spread[..., rows + width :], 1, 2)
    from_left = jnp.swapaxes(shifted_in(to_right, True), 1, 2)
    from_right = jnp.swapaxes(shifted_in(to_left, False), 1, 2)
    edges = jnp.concatenate(
        [from_left, jnp.zeros((batch_count, out_count, rows - 2 * width), jnp.float32), from_right],
        axis=2,
    )
    summed = spread[..., width : width + rows] + edges
    return inputs + summed + conv_bias[:, None]


def rotate(values, positions):
    half_width = values.shape[-1] // 2
    frequency = jnp.exp(
        -math.log(10000.0) * jnp.arange(half_width).astype(jnp.float32) / half_width
    )
    angle = positions[:, None] * frequency[None, :]
    cosine = jnp.cos(angle)
    sine_part = jnp.sin(angle)
    lower_half = values[..., :half_width]
    upper_half = values[..., half_width:]
    return jnp.concatenate(
        [
            lower_half * cosine - upper_half * sine_part,
            lower_half * sine_part + upper_half * cosine,
        ],
        axis=-1,
    )


LANES = 128


def packed(x):
    rows, width = x.shape[-2:]
    if (rows * width) % LANES:
        return x
    return x.reshape(x.shape[:-2] + (rows * width // LANES, LANES))


def unpacked(x, rows, width):
    return x.reshape(x.shape[:-2] + (rows, width))


def gathered_packed(x, axis_name):
    rows, width = x.shape[-2:]
    return unpacked(gathered(packed(x), axis_name), rows, width)


def head_attention(hidden_all, norm_gain, qkv_weight, positions):
    group = hidden_all.shape[0]
    attn_width = norm_gain.shape[0]
    squares = jnp.sum(hidden_all * hidden_all, axis=(0, 3))
    gain_blocks = norm_gain.reshape(group, 1, 1, attn_width // group)
    qkv_blocks = qkv_weight.reshape(group, attn_width // group, qkv_weight.shape[1])
    projected = jnp.einsum(
        "nbtj,njo->bto", hidden_all * gain_blocks, qkv_blocks, precision=MATMUL_PRECISION
    )
    root_mean = jnp.sqrt(squares / attn_width + 1e-06)
    projected = projected / root_mean[..., None]
    head_extent = qkv_weight.shape[1] // 3
    query_rows = rotate(projected[..., :head_extent], positions) / math.sqrt(head_extent)
    key_matrix = rotate(projected[..., head_extent : 2 * head_extent], positions)
    return query_rows, key_matrix, projected[..., 2 * head_extent :]


def attention_by_batch(pooled, up_weight, norm_gain, qkv_weight, out_weight):
    batch_count, pooled_rows, channels = pooled.shape
    seq = lax.axis_size("seq")
    group = lax.axis_size(CHANNELS)
    per = batch_count // seq
    length = seq * pooled_rows
    mine = lax.all_to_all(pooled.reshape(seq, per, pooled_rows, channels), "seq", 0, 0, tiled=True)
    mine = jnp.transpose(mine, (1, 0, 2, 3)).reshape(per, length, channels)
    pooled_all = gathered_packed(mine, CHANNELS)
    up_blocks = up_weight.reshape(up_weight.shape[0], group, channels)
    hidden = jnp.einsum("nbti,oni->bto", pooled_all, up_blocks, precision=MATMUL_PRECISION)
    hidden_all = gathered_packed(hidden, CHANNELS)
    positions = jnp.arange(length, dtype=jnp.int32).astype(jnp.float32)
    query_rows, key_matrix, value_matrix = head_attention(hidden_all, norm_gain, qkv_weight, positions)
    attention_scores = jnp.einsum(
        "btc,bxc->btx", query_rows, key_matrix, precision=MATMUL_PRECISION
    )
    top = jnp.max(attention_scores, axis=2)
    probabilities = jnp.exp(attention_scores - top[..., None])
    denominator = jnp.sum(probabilities, axis=2)
    weighted_values = jnp.einsum(
        "btx,bxe->bte", probabilities, value_matrix, precision=MATMUL_PRECISION
    )
    head_result = weighted_values / denominator[..., None]
    out_width = out_weight.shape[1] // group
    out_blocks = out_weight.reshape(out_weight.shape[0], group, out_width)
    shares = jnp.einsum("btd,dne->nbte", head_result, out_blocks, precision=MATMUL_PRECISION)
    summed = jnp.sum(lax.all_to_all(shares, CHANNELS, 0, 0, tiled=True), axis=0)
    by_block = jnp.transpose(summed.reshape(per, seq, pooled_rows, out_width), (1, 0, 2, 3))
    back = lax.all_to_all(packed(by_block), "seq", 0, 0, tiled=True)
    return unpacked(back, pooled_rows, out_width).reshape(batch_count, pooled_rows, out_width)


def attention_by_position(pooled, up_weight, norm_gain, qkv_weight, out_weight):
    batch_count, pooled_rows, channels = pooled.shape
    group = lax.axis_size(CHANNELS)
    pooled_all = gathered_packed(pooled, CHANNELS)
    up_blocks = up_weight.reshape(up_weight.shape[0], group, channels)
    hidden = jnp.einsum("nbti,oni->bto", pooled_all, up_blocks, precision=MATMUL_PRECISION)
    hidden_all = gathered_packed(hidden, CHANNELS)
    positions = (
        lax.axis_index("seq") * pooled_rows + jnp.arange(pooled_rows, dtype=jnp.int32)
    ).astype(jnp.float32)
    query_rows, key_matrix, value_matrix = head_attention(hidden_all, norm_gain, qkv_weight, positions)
    head_extent = query_rows.shape[-1]
    keys_and_values = jnp.concatenate([key_matrix, value_matrix], axis=2)
    kv_all = gathered(keys_and_values, "seq")
    attention_scores = jnp.einsum(
        "btc,nbxc->btnx", query_rows, kv_all[..., :head_extent], precision=MATMUL_PRECISION
    )
    top = jnp.max(attention_scores, axis=(2, 3))
    probabilities = jnp.exp(attention_scores - top[..., None, None])
    denominator = jnp.sum(probabilities, axis=(2, 3))
    weighted_values = jnp.einsum(
        "btnx,nbxe->bte", probabilities, kv_all[..., head_extent:], precision=MATMUL_PRECISION
    )
    head_result = weighted_values / denominator[..., None]
    out_width = out_weight.shape[1] // group
    out_blocks = out_weight.reshape(out_weight.shape[0], group, out_width)
    shares = jnp.einsum("btd,dne->nbte", head_result, out_blocks, precision=MATMUL_PRECISION)
    summed = jnp.sum(lax.all_to_all(packed(shares), CHANNELS, 0, 0, tiled=True), axis=0)
    return unpacked(summed, pooled_rows, out_width)


def per_device(
    features,
    first_channel_scale,
    first_channel_shift,
    first_conv_bias,
    first_kernel_taps,
    second_channel_scale,
    second_channel_shift,
    second_conv_bias,
    second_kernel_taps,
    up_weight,
    norm_gain,
    qkv_weight,
    out_weight,
):
    batch_count = features.shape[0]
    channels = features.shape[1]
    row_count = features.shape[2]
    first_part = convolution_block(
        features,
        first_channel_scale,
        first_channel_shift,
        first_conv_bias,
        first_kernel_taps,
        FIRST_DILATION,
    )
    tower_skip_output = convolution_block(
        first_part,
        second_channel_scale,
        second_channel_shift,
        second_conv_bias,
        second_kernel_taps,
        SECOND_DILATION,
    )
    pooled_rows = row_count // POOL
    pooled = jnp.transpose(
        jnp.max(tower_skip_output.reshape(batch_count, channels, pooled_rows, POOL), axis=3),
        (0, 2, 1),
    )
    if batch_count % lax.axis_size("seq") == 0:
        attended = attention_by_batch(pooled, up_weight, norm_gain, qkv_weight, out_weight)
    else:
        attended = attention_by_position(pooled, up_weight, norm_gain, qkv_weight, out_weight)
    return (tower_skip_output, attended)


def solution(mesh):
    placed = (
        P(None, CHANNELS, "seq"),
        P(CHANNELS),
        P(CHANNELS),
        P(CHANNELS),
        P(None, CHANNELS, None),
        P(CHANNELS),
        P(CHANNELS),
        P(CHANNELS),
        P(None, CHANNELS, None),
        P(CHANNELS, None),
        P(),
        P(None, CHANNELS),
        P(CHANNELS, None),
    )
    return jax.shard_map(
        per_device,
        mesh=mesh,
        in_specs=placed,
        out_specs=(P(None, CHANNELS, "seq"), P(None, "seq", CHANNELS)),
        check_vma=False,
    )
```

```python
import math

import jax
import jax.numpy as jnp
from jax import lax
from jax.sharding import PartitionSpec as P

FIRST_DILATION = 2
SECOND_DILATION = 4
POOL = 8
TAPS = 5

MATMUL_PRECISION = lax.Precision.HIGH
CHANNELS = ("crow", "ccol")


def gathered(x, axis_name):
    count = lax.axis_size(axis_name)
    copies = jnp.broadcast_to(x[None], (count,) + x.shape)
    return lax.all_to_all(copies, axis_name, 0, 0, tiled=True)


def summed_scatter(x, axis_name):
    return jnp.sum(lax.all_to_all(x, axis_name, 0, 0, tiled=True), axis=0)


def swap_ccol(x):
    return lax.ppermute(x, "ccol", [(0, 1), (1, 0)])


def shifted_in(edge, forward):
    count = lax.axis_size("seq")
    if forward:
        pairs = [(i, i + 1) for i in range(count - 1)]
    else:
        pairs = [(i + 1, i) for i in range(count - 1)]
    return lax.ppermute(edge, "seq", pairs)


def row_exchange(activated):
    pairs = lambda step: [(j, j ^ step) for j in range(4)]
    across = lax.ppermute(activated, "crow", pairs(1))
    along = lax.ppermute(activated, "crow", pairs(2))
    half = activated.shape[0] // 2
    first = lax.ppermute(across[:half], "crow", pairs(2))
    second = lax.ppermute(along[half:], "crow", pairs(1))
    diagonal = jnp.concatenate([first, second], axis=0)
    slots = [activated, across, along, diagonal]
    return jnp.stack(slots), jnp.stack([swap_ccol(one) for one in slots])


def convolution_block(inputs, bn_scale, bn_shift, conv_bias, kernel, dilation):
    activated = jax.nn.gelu(inputs * bn_scale[:, None] + bn_shift[:, None], approximate=False)
    core = lax.axis_index("ccol")
    if lax.axis_size("crow") == 4 and activated.shape[0] % 2 == 0:
        slots, other_slots = row_exchange(activated)
        row = lax.axis_index("crow")
        by_row = jnp.stack([jnp.take(slots, jnp.bitwise_xor(row, r), axis=0) for r in range(4)])
        other_core = jnp.stack([jnp.take(other_slots, jnp.bitwise_xor(row, r), axis=0) for r in range(4)])
    else:
        by_row = gathered(activated, "crow")
        other_core = swap_ccol(by_row)
    tap_count, out_count, in_count = kernel.shape
    row_count, batch_count, block, rows = by_row.shape
    slot = lax.broadcasted_iota(jnp.int32, (1, 2, 1, 1, 1), 1)
    ordered = jnp.where(slot == core, by_row[:, None], other_core[:, None])
    ordered = jnp.transpose(ordered, (2, 4, 0, 1, 3)).reshape(batch_count, rows, in_count)
    products = jnp.einsum("btc,koc->kbto", ordered, kernel, precision=MATMUL_PRECISION)
    batch_count, rows = inputs.shape[0], inputs.shape[2]
    width = 2 * dilation
    padded = jnp.pad(products, ((0, 0), (0, 0), (2 * width, 2 * width), (0, 0)))
    spread = None
    for tap_index in range(tap_count):
        offset = tap_index * dilation
        term = padded[tap_index, :, offset : offset + rows + 2 * width, :]
        spread = term if spread is None else spread + term
    spread = jnp.swapaxes(spread, 1, 2)
    to_left = jnp.swapaxes(spread[..., :width], 1, 2)
    to_right = jnp.swapaxes(spread[..., rows + width :], 1, 2)
    from_left = jnp.swapaxes(shifted_in(to_right, True), 1, 2)
    from_right = jnp.swapaxes(shifted_in(to_left, False), 1, 2)
    edges = jnp.concatenate(
        [from_left, jnp.zeros((batch_count, out_count, rows - 2 * width), jnp.float32), from_right],
        axis=2,
    )
    summed = spread[..., width : width + rows] + edges
    return inputs + summed + conv_bias[:, None]


def rotate(values, positions):
    half_width = values.shape[-1] // 2
    frequency = jnp.exp(
        -math.log(10000.0) * jnp.arange(half_width).astype(jnp.float32) / half_width
    )
    angle = positions[:, None] * frequency[None, :]
    cosine = jnp.cos(angle)
    sine_part = jnp.sin(angle)
    lower_half = values[..., :half_width]
    upper_half = values[..., half_width:]
    return jnp.concatenate(
        [
            lower_half * cosine - upper_half * sine_part,
            lower_half * sine_part + upper_half * cosine,
        ],
        axis=-1,
    )


LANES = 128


def packed(x):
    rows, width = x.shape[-2:]
    if (rows * width) % LANES:
        return x
    return x.reshape(x.shape[:-2] + (rows * width // LANES, LANES))


def unpacked(x, rows, width):
    return x.reshape(x.shape[:-2] + (rows, width))


def gathered_packed(x, axis_name):
    rows, width = x.shape[-2:]
    return unpacked(gathered(packed(x), axis_name), rows, width)


def head_attention(hidden_all, norm_gain, qkv_weight, positions):
    group = hidden_all.shape[0]
    attn_width = norm_gain.shape[0]
    squares = jnp.sum(hidden_all * hidden_all, axis=(0, 3))
    gain_blocks = norm_gain.reshape(group, 1, 1, attn_width // group)
    qkv_blocks = qkv_weight.reshape(group, attn_width // group, qkv_weight.shape[1])
    projected = jnp.einsum(
        "nbtj,njo->bto", hidden_all * gain_blocks, qkv_blocks, precision=MATMUL_PRECISION
    )
    root_mean = jnp.sqrt(squares / attn_width + 1e-06)
    projected = projected / root_mean[..., None]
    head_extent = qkv_weight.shape[1] // 3
    query_rows = rotate(projected[..., :head_extent], positions) / math.sqrt(head_extent)
    key_matrix = rotate(projected[..., head_extent : 2 * head_extent], positions)
    return query_rows, key_matrix, projected[..., 2 * head_extent :]


def attention_by_batch(pooled, up_weight, norm_gain, qkv_weight, out_weight):
    batch_count, pooled_rows, channels = pooled.shape
    seq = lax.axis_size("seq")
    group = lax.axis_size(CHANNELS)
    per = batch_count // seq
    length = seq * pooled_rows
    mine = lax.all_to_all(pooled.reshape(seq, per, pooled_rows, channels), "seq", 0, 0, tiled=True)
    mine = jnp.transpose(mine, (1, 0, 2, 3)).reshape(per, length, channels)
    pooled_all = gathered_packed(mine, CHANNELS)
    up_blocks = up_weight.reshape(up_weight.shape[0], group, channels)
    hidden = jnp.einsum("nbti,oni->bto", pooled_all, up_blocks, precision=MATMUL_PRECISION)
    hidden_all = gathered_packed(hidden, CHANNELS)
    positions = jnp.arange(length, dtype=jnp.int32).astype(jnp.float32)
    query_rows, key_matrix, value_matrix = head_attention(hidden_all, norm_gain, qkv_weight, positions)
    attention_scores = jnp.einsum(
        "btc,bxc->btx", query_rows, key_matrix, precision=MATMUL_PRECISION
    )
    top = jnp.max(attention_scores, axis=2)
    probabilities = jnp.exp(attention_scores - top[..., None])
    denominator = jnp.sum(probabilities, axis=2)
    weighted_values = jnp.einsum(
        "btx,bxe->bte", probabilities, value_matrix, precision=MATMUL_PRECISION
    )
    head_result = weighted_values / denominator[..., None]
    out_width = out_weight.shape[1] // group
    out_blocks = out_weight.reshape(out_weight.shape[0], group, out_width)
    shares = jnp.einsum("btd,dne->nbte", head_result, out_blocks, precision=MATMUL_PRECISION)
    summed = jnp.sum(lax.all_to_all(shares, CHANNELS, 0, 0, tiled=True), axis=0)
    by_block = jnp.transpose(summed.reshape(per, seq, pooled_rows, out_width), (1, 0, 2, 3))
    back = lax.all_to_all(packed(by_block), "seq", 0, 0, tiled=True)
    return unpacked(back, pooled_rows, out_width).reshape(batch_count, pooled_rows, out_width)


def attention_by_position(pooled, up_weight, norm_gain, qkv_weight, out_weight):
    batch_count, pooled_rows, channels = pooled.shape
    group = lax.axis_size(CHANNELS)
    pooled_all = gathered_packed(pooled, CHANNELS)
    up_blocks = up_weight.reshape(up_weight.shape[0], group, channels)
    hidden = jnp.einsum("nbti,oni->bto", pooled_all, up_blocks, precision=MATMUL_PRECISION)
    hidden_all = gathered_packed(hidden, CHANNELS)
    positions = (
        lax.axis_index("seq") * pooled_rows + jnp.arange(pooled_rows, dtype=jnp.int32)
    ).astype(jnp.float32)
    query_rows, key_matrix, value_matrix = head_attention(hidden_all, norm_gain, qkv_weight, positions)
    head_extent = query_rows.shape[-1]
    keys_and_values = jnp.concatenate([key_matrix, value_matrix], axis=2)
    kv_all = gathered(keys_and_values, "seq")
    attention_scores = jnp.einsum(
        "btc,nbxc->btnx", query_rows, kv_all[..., :head_extent], precision=MATMUL_PRECISION
    )
    top = jnp.max(attention_scores, axis=(2, 3))
    probabilities = jnp.exp(attention_scores - top[..., None, None])
    denominator = jnp.sum(probabilities, axis=(2, 3))
    weighted_values = jnp.einsum(
        "btnx,nbxe->bte", probabilities, kv_all[..., head_extent:], precision=MATMUL_PRECISION
    )
    head_result = weighted_values / denominator[..., None]
    out_width = out_weight.shape[1] // group
    out_blocks = out_weight.reshape(out_weight.shape[0], group, out_width)
    shares = jnp.einsum("btd,dne->nbte", head_result, out_blocks, precision=MATMUL_PRECISION)
    summed = jnp.sum(lax.all_to_all(packed(shares), CHANNELS, 0, 0, tiled=True), axis=0)
    return unpacked(summed, pooled_rows, out_width)


def per_device(
    features,
    first_channel_scale,
    first_channel_shift,
    first_conv_bias,
    first_kernel_taps,
    second_channel_scale,
    second_channel_shift,
    second_conv_bias,
    second_kernel_taps,
    up_weight,
    norm_gain,
    qkv_weight,
    out_weight,
):
    batch_count = features.shape[0]
    channels = features.shape[1]
    row_count = features.shape[2]
    first_part = convolution_block(
        features,
        first_channel_scale,
        first_channel_shift,
        first_conv_bias,
        first_kernel_taps,
        FIRST_DILATION,
    )
    tower_skip_output = convolution_block(
        first_part,
        second_channel_scale,
        second_channel_shift,
        second_conv_bias,
        second_kernel_taps,
        SECOND_DILATION,
    )
    pooled_rows = row_count // POOL
    pooled = jnp.transpose(
        jnp.max(tower_skip_output.reshape(batch_count, channels, pooled_rows, POOL), axis=3),
        (0, 2, 1),
    )
    if batch_count % lax.axis_size("seq") == 0:
        attended = attention_by_batch(pooled, up_weight, norm_gain, qkv_weight, out_weight)
    else:
        attended = attention_by_position(pooled, up_weight, norm_gain, qkv_weight, out_weight)
    return (tower_skip_output, attended)


def solution(mesh):
    placed = (
        P(None, CHANNELS, "seq"),
        P(CHANNELS),
        P(CHANNELS),
        P(CHANNELS),
        P(None, CHANNELS, None),
        P(CHANNELS),
        P(CHANNELS),
        P(CHANNELS),
        P(None, CHANNELS, None),
        P(CHANNELS, None),
        P(),
        P(None, CHANNELS),
        P(CHANNELS, None),
    )
    return jax.shard_map(
        per_device,
        mesh=mesh,
        in_specs=placed,
        out_specs=(P(None, CHANNELS, "seq"), P(None, "seq", CHANNELS)),
        check_vma=False,
    )
```

```python
import math

import jax
import jax.numpy as jnp
from jax import lax
from jax.sharding import PartitionSpec as P

FIRST_DILATION = 2
SECOND_DILATION = 4
POOL = 8
TAPS = 5

MATMUL_PRECISION = lax.Precision.HIGH
CHANNELS = ("crow", "ccol")


def gathered(x, axis_name):
    count = lax.axis_size(axis_name)
    copies = jnp.broadcast_to(x[None], (count,) + x.shape)
    return lax.all_to_all(copies, axis_name, 0, 0, tiled=True)


def summed_scatter(x, axis_name):
    return jnp.sum(lax.all_to_all(x, axis_name, 0, 0, tiled=True), axis=0)


def swap_ccol(x):
    return lax.ppermute(x, "ccol", [(0, 1), (1, 0)])


def shifted_in(edge, forward):
    count = lax.axis_size("seq")
    if forward:
        pairs = [(i, i + 1) for i in range(count - 1)]
    else:
        pairs = [(i + 1, i) for i in range(count - 1)]
    return lax.ppermute(edge, "seq", pairs)


def row_exchange(activated):
    pairs = lambda step: [(j, j ^ step) for j in range(4)]
    across = lax.ppermute(activated, "crow", pairs(1))
    along = lax.ppermute(activated, "crow", pairs(2))
    half = activated.shape[0] // 2
    first = lax.ppermute(across[:half], "crow", pairs(2))
    second = lax.ppermute(along[half:], "crow", pairs(1))
    diagonal = jnp.concatenate([first, second], axis=0)
    slots = [activated, across, along, diagonal]
    return jnp.stack(slots), jnp.stack([swap_ccol(one) for one in slots])


def activation(inputs, bn_scale, bn_shift):
    return jax.nn.gelu(inputs * bn_scale[:, None] + bn_shift[:, None], approximate=False)


def channel_gather(activated):
    if lax.axis_size("crow") == 4 and activated.shape[0] % 2 == 0:
        slots, other_slots = row_exchange(activated)
        row = lax.axis_index("crow")
        by_row = jnp.stack([jnp.take(slots, jnp.bitwise_xor(row, r), axis=0) for r in range(4)])
        other_core = jnp.stack([jnp.take(other_slots, jnp.bitwise_xor(row, r), axis=0) for r in range(4)])
        return by_row, other_core
    by_row = gathered(activated, "crow")
    return by_row, swap_ccol(by_row)


def in_kernel_order(own, other, order):
    core = lax.axis_index("ccol")
    slot = lax.broadcasted_iota(jnp.int32, (1, 2) + (1,) * (own.ndim - 1), 1)
    ordered = jnp.where(slot == core, own[:, None], other[:, None])
    ordered = jnp.transpose(ordered, order)
    return ordered.reshape(ordered.shape[:2] + (-1,))


def tap_spread(blocks, kernel, dilation, edges=None):
    by_row, other_core = blocks
    tap_count, out_count, in_count = kernel.shape
    row_count, batch_count, block, rows = by_row.shape
    ordered = in_kernel_order(by_row, other_core, (2, 4, 0, 1, 3))
    if edges is not None:
        edge = in_kernel_order(edges[0], edges[1], (2, 3, 0, 1, 4))
        reach = edge.shape[1] // 2
        ordered = jnp.concatenate(
            [edge[:, :reach], ordered[:, reach : rows - reach], edge[:, reach:]], axis=1
        )
    products = jnp.einsum("btc,koc->kbto", ordered, kernel, precision=MATMUL_PRECISION)
    width = 2 * dilation
    padded = jnp.pad(products, ((0, 0), (0, 0), (2 * width, 2 * width), (0, 0)))
    spread = None
    for tap_index in range(tap_count):
        offset = tap_index * dilation
        term = padded[tap_index, :, offset : offset + rows + 2 * width, :]
        spread = term if spread is None else spread + term
    to_left = spread[:, :width, :]
    to_right = spread[:, rows + width :, :]
    return jnp.swapaxes(spread[:, width : width + rows, :], 1, 2), to_left, to_right


def spilled_in(to_left, to_right):
    from_left = jnp.swapaxes(shifted_in(to_right, True), 1, 2)
    from_right = jnp.swapaxes(shifted_in(to_left, False), 1, 2)
    return from_left, from_right


def with_edges(interior, from_left, from_right):
    rows = interior.shape[2]
    width = from_left.shape[2]
    middle = jnp.zeros(interior.shape[:2] + (rows - 2 * width,), jnp.float32)
    return interior + jnp.concatenate([from_left, middle, from_right], axis=2)


def tower(features, first_layer, second_layer):
    scale_a, shift_a, bias_a, kernel_a, dilation_a = first_layer
    scale_b, shift_b, bias_b, kernel_b, dilation_b = second_layer
    rows = features.shape[2]
    activated = activation(features, scale_a, shift_a)
    interior, to_left, to_right = tap_spread(channel_gather(activated), kernel_a, dilation_a)
    unfinished = features + interior + bias_a[:, None]
    blocks = channel_gather(activation(unfinished, scale_b, shift_b))
    from_left, from_right = spilled_in(to_left, to_right)
    first_part = with_edges(unfinished, from_left, from_right)
    width = from_left.shape[2]
    edge_columns = jnp.concatenate([first_part[..., :width], first_part[..., rows - width :]], axis=2)
    edge_active = jnp.swapaxes(activation(edge_columns, scale_b, shift_b), 1, 2)
    edge_blocks = channel_gather(edge_active)
    interior, to_left, to_right = tap_spread(blocks, kernel_b, dilation_b, edge_blocks)
    from_left, from_right = spilled_in(to_left, to_right)
    return first_part + with_edges(interior, from_left, from_right) + bias_b[:, None]


def rotate(values, positions):
    half_width = values.shape[-1] // 2
    frequency = jnp.exp(
        -math.log(10000.0) * jnp.arange(half_width).astype(jnp.float32) / half_width
    )
    angle = positions[:, None] * frequency[None, :]
    cosine = jnp.cos(angle)
    sine_part = jnp.sin(angle)
    lower_half = values[..., :half_width]
    upper_half = values[..., half_width:]
    return jnp.concatenate(
        [
            lower_half * cosine - upper_half * sine_part,
            lower_half * sine_part + upper_half * cosine,
        ],
        axis=-1,
    )


LANES = 128


def packed(x):
    rows, width = x.shape[-2:]
    if (rows * width) % LANES:
        return x
    return x.reshape(x.shape[:-2] + (rows * width // LANES, LANES))


def unpacked(x, rows, width):
    return x.reshape(x.shape[:-2] + (rows, width))


def gathered_packed(x, axis_name):
    rows, width = x.shape[-2:]
    return unpacked(gathered(packed(x), axis_name), rows, width)


def head_attention(hidden_all, norm_gain, qkv_weight, positions):
    group = hidden_all.shape[0]
    attn_width = norm_gain.shape[0]
    squares = jnp.sum(hidden_all * hidden_all, axis=(0, 3))
    gain_blocks = norm_gain.reshape(group, 1, 1, attn_width // group)
    qkv_blocks = qkv_weight.reshape(group, attn_width // group, qkv_weight.shape[1])
    projected = jnp.einsum(
        "nbtj,njo->bto", hidden_all * gain_blocks, qkv_blocks, precision=MATMUL_PRECISION
    )
    root_mean = jnp.sqrt(squares / attn_width + 1e-06)
    projected = projected / root_mean[..., None]
    head_extent = qkv_weight.shape[1] // 3
    query_rows = rotate(projected[..., :head_extent], positions) / math.sqrt(head_extent)
    key_matrix = rotate(projected[..., head_extent : 2 * head_extent], positions)
    return query_rows, key_matrix, projected[..., 2 * head_extent :]


def attention_by_batch(pooled, up_weight, norm_gain, qkv_weight, out_weight):
    batch_count, pooled_rows, channels = pooled.shape
    seq = lax.axis_size("seq")
    group = lax.axis_size(CHANNELS)
    per = batch_count // seq
    length = seq * pooled_rows
    mine = lax.all_to_all(pooled.reshape(seq, per, pooled_rows, channels), "seq", 0, 0, tiled=True)
    mine = jnp.transpose(mine, (1, 0, 2, 3)).reshape(per, length, channels)
    pooled_all = gathered_packed(mine, CHANNELS)
    up_blocks = up_weight.reshape(up_weight.shape[0], group, channels)
    hidden = jnp.einsum("nbti,oni->bto", pooled_all, up_blocks, precision=MATMUL_PRECISION)
    hidden_all = gathered_packed(hidden, CHANNELS)
    positions = jnp.arange(length, dtype=jnp.int32).astype(jnp.float32)
    query_rows, key_matrix, value_matrix = head_attention(hidden_all, norm_gain, qkv_weight, positions)
    attention_scores = jnp.einsum(
        "btc,bxc->btx", query_rows, key_matrix, precision=MATMUL_PRECISION
    )
    top = jnp.max(attention_scores, axis=2)
    probabilities = jnp.exp(attention_scores - top[..., None])
    denominator = jnp.sum(probabilities, axis=2)
    weighted_values = jnp.einsum(
        "btx,bxe->bte", probabilities, value_matrix, precision=MATMUL_PRECISION
    )
    head_result = weighted_values / denominator[..., None]
    out_width = out_weight.shape[1] // group
    out_blocks = out_weight.reshape(out_weight.shape[0], group, out_width)
    shares = jnp.einsum("btd,dne->nbte", head_result, out_blocks, precision=MATMUL_PRECISION)
    summed = jnp.sum(lax.all_to_all(shares, CHANNELS, 0, 0, tiled=True), axis=0)
    by_block = jnp.transpose(summed.reshape(per, seq, pooled_rows, out_width), (1, 0, 2, 3))
    back = lax.all_to_all(packed(by_block), "seq", 0, 0, tiled=True)
    return unpacked(back, pooled_rows, out_width).reshape(batch_count, pooled_rows, out_width)


def attention_by_position(pooled, up_weight, norm_gain, qkv_weight, out_weight):
    batch_count, pooled_rows, channels = pooled.shape
    group = lax.axis_size(CHANNELS)
    pooled_all = gathered_packed(pooled, CHANNELS)
    up_blocks = up_weight.reshape(up_weight.shape[0], group, channels)
    hidden = jnp.einsum("nbti,oni->bto", pooled_all, up_blocks, precision=MATMUL_PRECISION)
    hidden_all = gathered_packed(hidden, CHANNELS)
    positions = (
        lax.axis_index("seq") * pooled_rows + jnp.arange(pooled_rows, dtype=jnp.int32)
    ).astype(jnp.float32)
    query_rows, key_matrix, value_matrix = head_attention(hidden_all, norm_gain, qkv_weight, positions)
    head_extent = query_rows.shape[-1]
    keys_and_values = jnp.concatenate([key_matrix, value_matrix], axis=2)
    kv_all = gathered(keys_and_values, "seq")
    attention_scores = jnp.einsum(
        "btc,nbxc->btnx", query_rows, kv_all[..., :head_extent], precision=MATMUL_PRECISION
    )
    top = jnp.max(attention_scores, axis=(2, 3))
    probabilities = jnp.exp(attention_scores - top[..., None, None])
    denominator = jnp.sum(probabilities, axis=(2, 3))
    weighted_values = jnp.einsum(
        "btnx,nbxe->bte", probabilities, kv_all[..., head_extent:], precision=MATMUL_PRECISION
    )
    head_result = weighted_values / denominator[..., None]
    out_width = out_weight.shape[1] // group
    out_blocks = out_weight.reshape(out_weight.shape[0], group, out_width)
    shares = jnp.einsum("btd,dne->nbte", head_result, out_blocks, precision=MATMUL_PRECISION)
    summed = jnp.sum(lax.all_to_all(packed(shares), CHANNELS, 0, 0, tiled=True), axis=0)
    return unpacked(summed, pooled_rows, out_width)


def per_device(
    features,
    first_channel_scale,
    first_channel_shift,
    first_conv_bias,
    first_kernel_taps,
    second_channel_scale,
    second_channel_shift,
    second_conv_bias,
    second_kernel_taps,
    up_weight,
    norm_gain,
    qkv_weight,
    out_weight,
):
    batch_count = features.shape[0]
    channels = features.shape[1]
    row_count = features.shape[2]
    tower_skip_output = tower(
        features,
        (first_channel_scale, first_channel_shift, first_conv_bias, first_kernel_taps, FIRST_DILATION),
        (second_channel_scale, second_channel_shift, second_conv_bias, second_kernel_taps, SECOND_DILATION),
    )
    pooled_rows = row_count // POOL
    pooled = jnp.transpose(
        jnp.max(tower_skip_output.reshape(batch_count, channels, pooled_rows, POOL), axis=3),
        (0, 2, 1),
    )
    if batch_count % lax.axis_size("seq") == 0:
        attended = attention_by_batch(pooled, up_weight, norm_gain, qkv_weight, out_weight)
    else:
        attended = attention_by_position(pooled, up_weight, norm_gain, qkv_weight, out_weight)
    return (tower_skip_output, attended)


def solution(mesh):
    placed = (
        P(None, CHANNELS, "seq"),
        P(CHANNELS),
        P(CHANNELS),
        P(CHANNELS),
        P(None, CHANNELS, None),
        P(CHANNELS),
        P(CHANNELS),
        P(CHANNELS),
        P(None, CHANNELS, None),
        P(CHANNELS, None),
        P(),
        P(None, CHANNELS),
        P(CHANNELS, None),
    )
    return jax.shard_map(
        per_device,
        mesh=mesh,
        in_specs=placed,
        out_specs=(P(None, CHANNELS, "seq"), P(None, "seq", CHANNELS)),
        check_vma=False,
    )
```

```python
import math

import jax
import jax.numpy as jnp
from jax import lax
from jax.sharding import PartitionSpec as P

FIRST_DILATION = 2
SECOND_DILATION = 4
POOL = 8
TAPS = 5

MATMUL_PRECISION = lax.Precision.HIGH
CHANNELS = ("crow", "ccol")


def gathered(x, axis_name):
    count = lax.axis_size(axis_name)
    copies = jnp.broadcast_to(x[None], (count,) + x.shape)
    return lax.all_to_all(copies, axis_name, 0, 0, tiled=True)


def summed_scatter(x, axis_name):
    return jnp.sum(lax.all_to_all(x, axis_name, 0, 0, tiled=True), axis=0)


def swap_ccol(x):
    return lax.ppermute(x, "ccol", [(0, 1), (1, 0)])


def shifted_in(edge, forward):
    count = lax.axis_size("seq")
    if forward:
        pairs = [(i, i + 1) for i in range(count - 1)]
    else:
        pairs = [(i + 1, i) for i in range(count - 1)]
    return lax.ppermute(edge, "seq", pairs)


def row_exchange(activated):
    pairs = lambda step: [(j, j ^ step) for j in range(4)]
    across = lax.ppermute(activated, "crow", pairs(1))
    along = lax.ppermute(activated, "crow", pairs(2))
    half = activated.shape[0] // 2
    first = lax.ppermute(across[:half], "crow", pairs(2))
    second = lax.ppermute(along[half:], "crow", pairs(1))
    diagonal = jnp.concatenate([first, second], axis=0)
    slots = [activated, across, along, diagonal]
    return jnp.stack(slots), jnp.stack([swap_ccol(one) for one in slots])


def activation(inputs, bn_scale, bn_shift):
    return jax.nn.gelu(inputs * bn_scale[:, None] + bn_shift[:, None], approximate=False)


def channel_gather(activated):
    if lax.axis_size("crow") == 4 and activated.shape[0] % 2 == 0:
        slots, other_slots = row_exchange(activated)
        row = lax.axis_index("crow")
        by_row = jnp.stack([jnp.take(slots, jnp.bitwise_xor(row, r), axis=0) for r in range(4)])
        other_core = jnp.stack([jnp.take(other_slots, jnp.bitwise_xor(row, r), axis=0) for r in range(4)])
    else:
        by_row = gathered(activated, "crow")
        other_core = swap_ccol(by_row)
    return by_row, other_core


def tap_spread(by_row, other_core, kernel, dilation):
    core = lax.axis_index("ccol")
    tap_count, out_count, in_count = kernel.shape
    row_count, batch_count, block, rows = by_row.shape
    slot = lax.broadcasted_iota(jnp.int32, (1, 2, 1, 1, 1), 1)
    ordered = jnp.where(slot == core, by_row[:, None], other_core[:, None])
    ordered = jnp.transpose(ordered, (2, 4, 0, 1, 3)).reshape(batch_count, rows, in_count)
    products = jnp.einsum("btc,koc->kbto", ordered, kernel, precision=MATMUL_PRECISION)
    width = 2 * dilation
    padded = jnp.pad(products, ((0, 0), (0, 0), (2 * width, 2 * width), (0, 0)))
    spread = None
    for tap_index in range(tap_count):
        offset = tap_index * dilation
        term = padded[tap_index, :, offset : offset + rows + 2 * width, :]
        spread = term if spread is None else spread + term
    spread = jnp.swapaxes(spread, 1, 2)
    to_left = jnp.swapaxes(spread[..., :width], 1, 2)
    to_right = jnp.swapaxes(spread[..., rows + width :], 1, 2)
    return spread[..., width : width + rows], to_left, to_right


def spilled_in(to_left, to_right):
    from_left = jnp.swapaxes(shifted_in(to_right, True), 1, 2)
    from_right = jnp.swapaxes(shifted_in(to_left, False), 1, 2)
    return from_left, from_right


def with_edges(interior, from_left, from_right):
    rows = interior.shape[2]
    width = from_left.shape[2]
    middle = jnp.zeros(interior.shape[:2] + (rows - 2 * width,), jnp.float32)
    return interior + jnp.concatenate([from_left, middle, from_right], axis=2)


def patched(block, edges):
    rows = block.shape[-1]
    width = edges.shape[-1] // 2
    pad = [(0, 0)] * (block.ndim - 1)
    left = jnp.pad(edges[..., :width], pad + [(0, rows - width)])
    right = jnp.pad(edges[..., width:], pad + [(rows - width, 0)])
    column = lax.broadcasted_iota(jnp.int32, block.shape, block.ndim - 1)
    return jnp.where(column < width, left, jnp.where(column >= rows - width, right, block))


def tower(features, first_layer, second_layer):
    scale_a, shift_a, bias_a, kernel_a, dilation_a = first_layer
    scale_b, shift_b, bias_b, kernel_b, dilation_b = second_layer
    rows = features.shape[2]
    interior, to_left, to_right = tap_spread(
        *channel_gather(activation(features, scale_a, shift_a)), kernel_a, dilation_a
    )
    unfinished = features + interior + bias_a[:, None]
    by_row, other_core = channel_gather(activation(unfinished, scale_b, shift_b))
    from_left, from_right = spilled_in(to_left, to_right)
    first_part = with_edges(unfinished, from_left, from_right)
    width = from_left.shape[2]
    edge_columns = jnp.concatenate([first_part[..., :width], first_part[..., rows - width :]], axis=2)
    edge_active = jnp.swapaxes(activation(edge_columns, scale_b, shift_b), 1, 2)
    edge_own, edge_other = channel_gather(edge_active)
    by_row = patched(by_row, jnp.swapaxes(edge_own, -1, -2))
    other_core = patched(other_core, jnp.swapaxes(edge_other, -1, -2))
    interior, to_left, to_right = tap_spread(by_row, other_core, kernel_b, dilation_b)
    from_left, from_right = spilled_in(to_left, to_right)
    return first_part + with_edges(interior, from_left, from_right) + bias_b[:, None]


def rotate(values, positions):
    half_width = values.shape[-1] // 2
    frequency = jnp.exp(
        -math.log(10000.0) * jnp.arange(half_width).astype(jnp.float32) / half_width
    )
    angle = positions[:, None] * frequency[None, :]
    cosine = jnp.cos(angle)
    sine_part = jnp.sin(angle)
    lower_half = values[..., :half_width]
    upper_half = values[..., half_width:]
    return jnp.concatenate(
        [
            lower_half * cosine - upper_half * sine_part,
            lower_half * sine_part + upper_half * cosine,
        ],
        axis=-1,
    )


LANES = 128


def packed(x):
    rows, width = x.shape[-2:]
    if (rows * width) % LANES:
        return x
    return x.reshape(x.shape[:-2] + (rows * width // LANES, LANES))


def unpacked(x, rows, width):
    return x.reshape(x.shape[:-2] + (rows, width))


def gathered_packed(x, axis_name):
    rows, width = x.shape[-2:]
    return unpacked(gathered(packed(x), axis_name), rows, width)


def head_attention(hidden_all, norm_gain, qkv_weight, positions):
    group = hidden_all.shape[0]
    attn_width = norm_gain.shape[0]
    squares = jnp.sum(hidden_all * hidden_all, axis=(0, 3))
    gain_blocks = norm_gain.reshape(group, 1, 1, attn_width // group)
    qkv_blocks = qkv_weight.reshape(group, attn_width // group, qkv_weight.shape[1])
    projected = jnp.einsum(
        "nbtj,njo->bto", hidden_all * gain_blocks, qkv_blocks, precision=MATMUL_PRECISION
    )
    root_mean = jnp.sqrt(squares / attn_width + 1e-06)
    projected = projected / root_mean[..., None]
    head_extent = qkv_weight.shape[1] // 3
    query_rows = rotate(projected[..., :head_extent], positions) / math.sqrt(head_extent)
    key_matrix = rotate(projected[..., head_extent : 2 * head_extent], positions)
    return query_rows, key_matrix, projected[..., 2 * head_extent :]


def attention_by_batch(pooled, up_weight, norm_gain, qkv_weight, out_weight):
    batch_count, pooled_rows, channels = pooled.shape
    seq = lax.axis_size("seq")
    group = lax.axis_size(CHANNELS)
    per = batch_count // seq
    length = seq * pooled_rows
    mine = lax.all_to_all(pooled.reshape(seq, per, pooled_rows, channels), "seq", 0, 0, tiled=True)
    mine = jnp.transpose(mine, (1, 0, 2, 3)).reshape(per, length, channels)
    pooled_all = gathered_packed(mine, CHANNELS)
    up_blocks = up_weight.reshape(up_weight.shape[0], group, channels)
    hidden = jnp.einsum("nbti,oni->bto", pooled_all, up_blocks, precision=MATMUL_PRECISION)
    hidden_all = gathered_packed(hidden, CHANNELS)
    positions = jnp.arange(length, dtype=jnp.int32).astype(jnp.float32)
    query_rows, key_matrix, value_matrix = head_attention(hidden_all, norm_gain, qkv_weight, positions)
    attention_scores = jnp.einsum(
        "btc,bxc->btx", query_rows, key_matrix, precision=MATMUL_PRECISION
    )
    top = jnp.max(attention_scores, axis=2)
    probabilities = jnp.exp(attention_scores - top[..., None])
    denominator = jnp.sum(probabilities, axis=2)
    weighted_values = jnp.einsum(
        "btx,bxe->bte", probabilities, value_matrix, precision=MATMUL_PRECISION
    )
    head_result = weighted_values / denominator[..., None]
    out_width = out_weight.shape[1] // group
    out_blocks = out_weight.reshape(out_weight.shape[0], group, out_width)
    shares = jnp.einsum("btd,dne->nbte", head_result, out_blocks, precision=MATMUL_PRECISION)
    summed = jnp.sum(lax.all_to_all(shares, CHANNELS, 0, 0, tiled=True), axis=0)
    by_block = jnp.transpose(summed.reshape(per, seq, pooled_rows, out_width), (1, 0, 2, 3))
    back = lax.all_to_all(packed(by_block), "seq", 0, 0, tiled=True)
    return unpacked(back, pooled_rows, out_width).reshape(batch_count, pooled_rows, out_width)


def attention_by_position(pooled, up_weight, norm_gain, qkv_weight, out_weight):
    batch_count, pooled_rows, channels = pooled.shape
    group = lax.axis_size(CHANNELS)
    pooled_all = gathered_packed(pooled, CHANNELS)
    up_blocks = up_weight.reshape(up_weight.shape[0], group, channels)
    hidden = jnp.einsum("nbti,oni->bto", pooled_all, up_blocks, precision=MATMUL_PRECISION)
    hidden_all = gathered_packed(hidden, CHANNELS)
    positions = (
        lax.axis_index("seq") * pooled_rows + jnp.arange(pooled_rows, dtype=jnp.int32)
    ).astype(jnp.float32)
    query_rows, key_matrix, value_matrix = head_attention(hidden_all, norm_gain, qkv_weight, positions)
    head_extent = query_rows.shape[-1]
    keys_and_values = jnp.concatenate([key_matrix, value_matrix], axis=2)
    kv_all = gathered(keys_and_values, "seq")
    attention_scores = jnp.einsum(
        "btc,nbxc->btnx", query_rows, kv_all[..., :head_extent], precision=MATMUL_PRECISION
    )
    top = jnp.max(attention_scores, axis=(2, 3))
    probabilities = jnp.exp(attention_scores - top[..., None, None])
    denominator = jnp.sum(probabilities, axis=(2, 3))
    weighted_values = jnp.einsum(
        "btnx,nbxe->bte", probabilities, kv_all[..., head_extent:], precision=MATMUL_PRECISION
    )
    head_result = weighted_values / denominator[..., None]
    out_width = out_weight.shape[1] // group
    out_blocks = out_weight.reshape(out_weight.shape[0], group, out_width)
    shares = jnp.einsum("btd,dne->nbte", head_result, out_blocks, precision=MATMUL_PRECISION)
    summed = jnp.sum(lax.all_to_all(packed(shares), CHANNELS, 0, 0, tiled=True), axis=0)
    return unpacked(summed, pooled_rows, out_width)


def per_device(
    features,
    first_channel_scale,
    first_channel_shift,
    first_conv_bias,
    first_kernel_taps,
    second_channel_scale,
    second_channel_shift,
    second_conv_bias,
    second_kernel_taps,
    up_weight,
    norm_gain,
    qkv_weight,
    out_weight,
):
    batch_count = features.shape[0]
    channels = features.shape[1]
    row_count = features.shape[2]
    tower_skip_output = tower(
        features,
        (first_channel_scale, first_channel_shift, first_conv_bias, first_kernel_taps, FIRST_DILATION),
        (second_channel_scale, second_channel_shift, second_conv_bias, second_kernel_taps, SECOND_DILATION),
    )
    pooled_rows = row_count // POOL
    pooled = jnp.transpose(
        jnp.max(tower_skip_output.reshape(batch_count, channels, pooled_rows, POOL), axis=3),
        (0, 2, 1),
    )
    if batch_count % lax.axis_size("seq") == 0:
        attended = attention_by_batch(pooled, up_weight, norm_gain, qkv_weight, out_weight)
    else:
        attended = attention_by_position(pooled, up_weight, norm_gain, qkv_weight, out_weight)
    return (tower_skip_output, attended)


def solution(mesh):
    placed = (
        P(None, CHANNELS, "seq"),
        P(CHANNELS),
        P(CHANNELS),
        P(CHANNELS),
        P(None, CHANNELS, None),
        P(CHANNELS),
        P(CHANNELS),
        P(CHANNELS),
        P(None, CHANNELS, None),
        P(CHANNELS, None),
        P(),
        P(None, CHANNELS),
        P(CHANNELS, None),
    )
    return jax.shard_map(
        per_device,
        mesh=mesh,
        in_specs=placed,
        out_specs=(P(None, CHANNELS, "seq"), P(None, "seq", CHANNELS)),
        check_vma=False,
    )
```

```python
import math

import jax
import jax.numpy as jnp
from jax import lax
from jax.sharding import PartitionSpec as P

FIRST_DILATION = 2
SECOND_DILATION = 4
POOL = 8
TAPS = 5

MATMUL_PRECISION = lax.Precision.HIGH
CHANNELS = ("crow", "ccol")


def gathered(x, axis_name):
    count = lax.axis_size(axis_name)
    copies = jnp.broadcast_to(x[None], (count,) + x.shape)
    return lax.all_to_all(copies, axis_name, 0, 0, tiled=True)


def summed_scatter(x, axis_name):
    return jnp.sum(lax.all_to_all(x, axis_name, 0, 0, tiled=True), axis=0)


def swap_ccol(x):
    return lax.ppermute(x, "ccol", [(0, 1), (1, 0)])


def shifted_in(edge, forward):
    count = lax.axis_size("seq")
    if forward:
        pairs = [(i, i + 1) for i in range(count - 1)]
    else:
        pairs = [(i + 1, i) for i in range(count - 1)]
    return lax.ppermute(edge, "seq", pairs)


def row_exchange(activated):
    pairs = lambda step: [(j, j ^ step) for j in range(4)]
    across = lax.ppermute(activated, "crow", pairs(1))
    along = lax.ppermute(activated, "crow", pairs(2))
    half = activated.shape[0] // 2
    first = lax.ppermute(across[:half], "crow", pairs(2))
    second = lax.ppermute(along[half:], "crow", pairs(1))
    diagonal = jnp.concatenate([first, second], axis=0)
    slots = [activated, across, along, diagonal]
    return jnp.stack(slots), jnp.stack([swap_ccol(one) for one in slots])


def convolution_block(inputs, bn_scale, bn_shift, conv_bias, kernel, dilation):
    activated = jax.nn.gelu(inputs * bn_scale[:, None] + bn_shift[:, None], approximate=False)
    core = lax.axis_index("ccol")
    if lax.axis_size("crow") == 4 and activated.shape[0] % 2 == 0:
        slots, other_slots = row_exchange(activated)
        row = lax.axis_index("crow")
        by_row = jnp.stack([jnp.take(slots, jnp.bitwise_xor(row, r), axis=0) for r in range(4)])
        other_core = jnp.stack([jnp.take(other_slots, jnp.bitwise_xor(row, r), axis=0) for r in range(4)])
    else:
        by_row = gathered(activated, "crow")
        other_core = swap_ccol(by_row)
    tap_count, out_count, in_count = kernel.shape
    row_count, batch_count, block, rows = by_row.shape
    slot = lax.broadcasted_iota(jnp.int32, (1, 2, 1, 1, 1), 1)
    ordered = jnp.where(slot == core, by_row[:, None], other_core[:, None])
    ordered = jnp.transpose(ordered, (2, 4, 0, 1, 3)).reshape(batch_count, rows, in_count)
    products = jnp.einsum("btc,koc->kbto", ordered, kernel, precision=MATMUL_PRECISION)
    batch_count, rows = inputs.shape[0], inputs.shape[2]
    width = 2 * dilation
    padded = jnp.pad(products, ((0, 0), (0, 0), (2 * width, 2 * width), (0, 0)))
    spread = None
    for tap_index in range(tap_count):
        offset = tap_index * dilation
        term = padded[tap_index, :, offset : offset + rows + 2 * width, :]
        spread = term if spread is None else spread + term
    spread = jnp.swapaxes(spread, 1, 2)
    to_left = jnp.swapaxes(spread[..., :width], 1, 2)
    to_right = jnp.swapaxes(spread[..., rows + width :], 1, 2)
    from_left = jnp.swapaxes(shifted_in(to_right, True), 1, 2)
    from_right = jnp.swapaxes(shifted_in(to_left, False), 1, 2)
    edges = jnp.concatenate(
        [from_left, jnp.zeros((batch_count, out_count, rows - 2 * width), jnp.float32), from_right],
        axis=2,
    )
    summed = spread[..., width : width + rows] + edges
    return inputs + summed + conv_bias[:, None]


def rotate(values, positions):
    half_width = values.shape[-1] // 2
    frequency = jnp.exp(
        -math.log(10000.0) * jnp.arange(half_width).astype(jnp.float32) / half_width
    )
    angle = positions[:, None] * frequency[None, :]
    cosine = jnp.cos(angle)
    sine_part = jnp.sin(angle)
    lower_half = values[..., :half_width]
    upper_half = values[..., half_width:]
    return jnp.concatenate(
        [
            lower_half * cosine - upper_half * sine_part,
            lower_half * sine_part + upper_half * cosine,
        ],
        axis=-1,
    )


LANES = 128


def packed(x):
    rows, width = x.shape[-2:]
    if (rows * width) % LANES:
        return x
    return x.reshape(x.shape[:-2] + (rows * width // LANES, LANES))


def unpacked(x, rows, width):
    return x.reshape(x.shape[:-2] + (rows, width))


def gathered_packed(x, axis_name):
    rows, width = x.shape[-2:]
    return unpacked(gathered(packed(x), axis_name), rows, width)


def head_attention(hidden_all, norm_gain, qkv_weight, positions):
    group = hidden_all.shape[0]
    attn_width = norm_gain.shape[0]
    squares = jnp.sum(hidden_all * hidden_all, axis=(0, 3))
    gain_blocks = norm_gain.reshape(group, 1, 1, attn_width // group)
    qkv_blocks = qkv_weight.reshape(group, attn_width // group, qkv_weight.shape[1])
    projected = jnp.einsum(
        "nbtj,njo->bto", hidden_all * gain_blocks, qkv_blocks, precision=MATMUL_PRECISION
    )
    root_mean = jnp.sqrt(squares / attn_width + 1e-06)
    projected = projected / root_mean[..., None]
    head_extent = qkv_weight.shape[1] // 3
    query_rows = rotate(projected[..., :head_extent], positions) / math.sqrt(head_extent)
    key_matrix = rotate(projected[..., head_extent : 2 * head_extent], positions)
    return query_rows, key_matrix, projected[..., 2 * head_extent :]


def channels_stacked(x):
    if lax.axis_size("crow") != 4 or x.shape[0] % 2:
        return gathered_packed(x, CHANNELS)
    slots, other_slots = row_exchange(x)
    row = lax.axis_index("crow")
    by_row = jnp.stack([jnp.take(slots, jnp.bitwise_xor(row, r), axis=0) for r in range(4)])
    other_core = jnp.stack([jnp.take(other_slots, jnp.bitwise_xor(row, r), axis=0) for r in range(4)])
    core = lax.axis_index("ccol")
    slot = lax.broadcasted_iota(jnp.int32, (1, 2) + (1,) * x.ndim, 1)
    both = jnp.where(slot == core, by_row[:, None], other_core[:, None])
    return both.reshape((-1,) + x.shape)


def attention_by_batch(pooled, up_weight, norm_gain, qkv_weight, out_weight):
    batch_count, pooled_rows, channels = pooled.shape
    seq = lax.axis_size("seq")
    group = lax.axis_size(CHANNELS)
    per = batch_count // seq
    length = seq * pooled_rows
    mine = lax.all_to_all(pooled.reshape(seq, per, pooled_rows, channels), "seq", 0, 0, tiled=True)
    mine = jnp.transpose(mine, (1, 0, 2, 3)).reshape(per, length, channels)
    pooled_all = channels_stacked(mine)
    up_blocks = up_weight.reshape(up_weight.shape[0], group, channels)
    hidden = jnp.einsum("nbti,oni->bto", pooled_all, up_blocks, precision=MATMUL_PRECISION)
    hidden_all = channels_stacked(hidden)
    positions = jnp.arange(length, dtype=jnp.int32).astype(jnp.float32)
    query_rows, key_matrix, value_matrix = head_attention(hidden_all, norm_gain, qkv_weight, positions)
    attention_scores = jnp.einsum(
        "btc,bxc->btx", query_rows, key_matrix, precision=MATMUL_PRECISION
    )
    top = jnp.max(attention_scores, axis=2)
    probabilities = jnp.exp(attention_scores - top[..., None])
    denominator = jnp.sum(probabilities, axis=2)
    weighted_values = jnp.einsum(
        "btx,bxe->bte", probabilities, value_matrix, precision=MATMUL_PRECISION
    )
    head_result = weighted_values / denominator[..., None]
    out_width = out_weight.shape[1] // group
    out_blocks = out_weight.reshape(out_weight.shape[0], group, out_width)
    shares = jnp.einsum("btd,dne->nbte", head_result, out_blocks, precision=MATMUL_PRECISION)
    summed = jnp.sum(lax.all_to_all(shares, CHANNELS, 0, 0, tiled=True), axis=0)
    by_block = jnp.transpose(summed.reshape(per, seq, pooled_rows, out_width), (1, 0, 2, 3))
    back = lax.all_to_all(packed(by_block), "seq", 0, 0, tiled=True)
    return unpacked(back, pooled_rows, out_width).reshape(batch_count, pooled_rows, out_width)


def attention_by_position(pooled, up_weight, norm_gain, qkv_weight, out_weight):
    batch_count, pooled_rows, channels = pooled.shape
    group = lax.axis_size(CHANNELS)
    pooled_all = gathered_packed(pooled, CHANNELS)
    up_blocks = up_weight.reshape(up_weight.shape[0], group, channels)
    hidden = jnp.einsum("nbti,oni->bto", pooled_all, up_blocks, precision=MATMUL_PRECISION)
    hidden_all = gathered_packed(hidden, CHANNELS)
    positions = (
        lax.axis_index("seq") * pooled_rows + jnp.arange(pooled_rows, dtype=jnp.int32)
    ).astype(jnp.float32)
    query_rows, key_matrix, value_matrix = head_attention(hidden_all, norm_gain, qkv_weight, positions)
    head_extent = query_rows.shape[-1]
    keys_and_values = jnp.concatenate([key_matrix, value_matrix], axis=2)
    kv_all = gathered(keys_and_values, "seq")
    attention_scores = jnp.einsum(
        "btc,nbxc->btnx", query_rows, kv_all[..., :head_extent], precision=MATMUL_PRECISION
    )
    top = jnp.max(attention_scores, axis=(2, 3))
    probabilities = jnp.exp(attention_scores - top[..., None, None])
    denominator = jnp.sum(probabilities, axis=(2, 3))
    weighted_values = jnp.einsum(
        "btnx,nbxe->bte", probabilities, kv_all[..., head_extent:], precision=MATMUL_PRECISION
    )
    head_result = weighted_values / denominator[..., None]
    out_width = out_weight.shape[1] // group
    out_blocks = out_weight.reshape(out_weight.shape[0], group, out_width)
    shares = jnp.einsum("btd,dne->nbte", head_result, out_blocks, precision=MATMUL_PRECISION)
    summed = jnp.sum(lax.all_to_all(packed(shares), CHANNELS, 0, 0, tiled=True), axis=0)
    return unpacked(summed, pooled_rows, out_width)


def per_device(
    features,
    first_channel_scale,
    first_channel_shift,
    first_conv_bias,
    first_kernel_taps,
    second_channel_scale,
    second_channel_shift,
    second_conv_bias,
    second_kernel_taps,
    up_weight,
    norm_gain,
    qkv_weight,
    out_weight,
):
    batch_count = features.shape[0]
    channels = features.shape[1]
    row_count = features.shape[2]
    first_part = convolution_block(
        features,
        first_channel_scale,
        first_channel_shift,
        first_conv_bias,
        first_kernel_taps,
        FIRST_DILATION,
    )
    tower_skip_output = convolution_block(
        first_part,
        second_channel_scale,
        second_channel_shift,
        second_conv_bias,
        second_kernel_taps,
        SECOND_DILATION,
    )
    pooled_rows = row_count // POOL
    pooled = jnp.transpose(
        jnp.max(tower_skip_output.reshape(batch_count, channels, pooled_rows, POOL), axis=3),
        (0, 2, 1),
    )
    if batch_count % lax.axis_size("seq") == 0:
        attended = attention_by_batch(pooled, up_weight, norm_gain, qkv_weight, out_weight)
    else:
        attended = attention_by_position(pooled, up_weight, norm_gain, qkv_weight, out_weight)
    return (tower_skip_output, attended)


def solution(mesh):
    placed = (
        P(None, CHANNELS, "seq"),
        P(CHANNELS),
        P(CHANNELS),
        P(CHANNELS),
        P(None, CHANNELS, None),
        P(CHANNELS),
        P(CHANNELS),
        P(CHANNELS),
        P(None, CHANNELS, None),
        P(CHANNELS, None),
        P(),
        P(None, CHANNELS),
        P(CHANNELS, None),
    )
    return jax.shard_map(
        per_device,
        mesh=mesh,
        in_specs=placed,
        out_specs=(P(None, CHANNELS, "seq"), P(None, "seq", CHANNELS)),
        check_vma=False,
    )
```

```python
import math

import jax
import jax.numpy as jnp
from jax import lax
from jax.sharding import PartitionSpec as P

FIRST_DILATION = 2
SECOND_DILATION = 4
POOL = 8
TAPS = 5

MATMUL_PRECISION = lax.Precision.HIGH
CHANNELS = ("crow", "ccol")


def gathered(x, axis_name):
    count = lax.axis_size(axis_name)
    copies = jnp.broadcast_to(x[None], (count,) + x.shape)
    return lax.all_to_all(copies, axis_name, 0, 0, tiled=True)


def summed_scatter(x, axis_name):
    return jnp.sum(lax.all_to_all(x, axis_name, 0, 0, tiled=True), axis=0)


def swap_ccol(x):
    return lax.ppermute(x, "ccol", [(0, 1), (1, 0)])


def shifted_in(edge, forward):
    count = lax.axis_size("seq")
    if forward:
        pairs = [(i, i + 1) for i in range(count - 1)]
    else:
        pairs = [(i + 1, i) for i in range(count - 1)]
    return lax.ppermute(edge, "seq", pairs)


def row_exchange(activated):
    pairs = lambda step: [(j, j ^ step) for j in range(4)]
    across = lax.ppermute(activated, "crow", pairs(1))
    along = lax.ppermute(activated, "crow", pairs(2))
    half = activated.shape[0] // 2
    first = lax.ppermute(across[:half], "crow", pairs(2))
    second = lax.ppermute(along[half:], "crow", pairs(1))
    diagonal = jnp.concatenate([first, second], axis=0)
    slots = [activated, across, along, diagonal]
    return jnp.stack(slots), jnp.stack([swap_ccol(one) for one in slots])


def convolution_block(inputs, bn_scale, bn_shift, conv_bias, kernel, dilation):
    activated = jax.nn.gelu(inputs * bn_scale[:, None] + bn_shift[:, None], approximate=False)
    core = lax.axis_index("ccol")
    if lax.axis_size("crow") == 4 and activated.shape[0] % 2 == 0:
        slots, other_slots = row_exchange(activated)
        row = lax.axis_index("crow")
        by_row = jnp.stack([jnp.take(slots, jnp.bitwise_xor(row, r), axis=0) for r in range(4)])
        other_core = jnp.stack([jnp.take(other_slots, jnp.bitwise_xor(row, r), axis=0) for r in range(4)])
    else:
        by_row = gathered(activated, "crow")
        other_core = swap_ccol(by_row)
    tap_count, out_count, in_count = kernel.shape
    row_count, batch_count, block, rows = by_row.shape
    slot = lax.broadcasted_iota(jnp.int32, (1, 2, 1, 1, 1), 1)
    ordered = jnp.where(slot == core, by_row[:, None], other_core[:, None])
    ordered = jnp.transpose(ordered, (2, 4, 0, 1, 3)).reshape(batch_count, rows, in_count)
    products = jnp.einsum("btc,koc->kbto", ordered, kernel, precision=MATMUL_PRECISION)
    batch_count, rows = inputs.shape[0], inputs.shape[2]
    width = 2 * dilation
    padded = jnp.pad(products, ((0, 0), (0, 0), (2 * width, 2 * width), (0, 0)))
    spread = None
    for tap_index in range(tap_count):
        offset = tap_index * dilation
        term = padded[tap_index, :, offset : offset + rows + 2 * width, :]
        spread = term if spread is None else spread + term
    spread = jnp.swapaxes(spread, 1, 2)
    to_left = jnp.swapaxes(spread[..., :width], 1, 2)
    to_right = jnp.swapaxes(spread[..., rows + width :], 1, 2)
    from_left = jnp.swapaxes(shifted_in(to_right, True), 1, 2)
    from_right = jnp.swapaxes(shifted_in(to_left, False), 1, 2)
    edges = jnp.concatenate(
        [from_left, jnp.zeros((batch_count, out_count, rows - 2 * width), jnp.float32), from_right],
        axis=2,
    )
    summed = spread[..., width : width + rows] + edges
    return inputs + summed + conv_bias[:, None]


def rotate(values, positions):
    half_width = values.shape[-1] // 2
    frequency = jnp.exp(
        -math.log(10000.0) * jnp.arange(half_width).astype(jnp.float32) / half_width
    )
    angle = positions[:, None] * frequency[None, :]
    cosine = jnp.cos(angle)
    sine_part = jnp.sin(angle)
    lower_half = values[..., :half_width]
    upper_half = values[..., half_width:]
    return jnp.concatenate(
        [
            lower_half * cosine - upper_half * sine_part,
            lower_half * sine_part + upper_half * cosine,
        ],
        axis=-1,
    )


LANES = 128


def packed(x):
    rows, width = x.shape[-2:]
    if (rows * width) % LANES:
        return x
    return x.reshape(x.shape[:-2] + (rows * width // LANES, LANES))


def unpacked(x, rows, width):
    return x.reshape(x.shape[:-2] + (rows, width))


def gathered_packed(x, axis_name):
    rows, width = x.shape[-2:]
    return unpacked(gathered(packed(x), axis_name), rows, width)


def head_attention(hidden_all, norm_gain, qkv_weight, positions):
    group = hidden_all.shape[0]
    attn_width = norm_gain.shape[0]
    squares = jnp.sum(hidden_all * hidden_all, axis=(0, 3))
    gain_blocks = norm_gain.reshape(group, 1, 1, attn_width // group)
    qkv_blocks = qkv_weight.reshape(group, attn_width // group, qkv_weight.shape[1])
    projected = jnp.einsum(
        "nbtj,njo->bto", hidden_all * gain_blocks, qkv_blocks, precision=MATMUL_PRECISION
    )
    root_mean = jnp.sqrt(squares / attn_width + 1e-06)
    projected = projected / root_mean[..., None]
    head_extent = qkv_weight.shape[1] // 3
    query_rows = rotate(projected[..., :head_extent], positions) / math.sqrt(head_extent)
    key_matrix = rotate(projected[..., head_extent : 2 * head_extent], positions)
    return query_rows, key_matrix, projected[..., 2 * head_extent :]


def seq_exchange(x):
    count = lax.axis_size("seq")
    me = lax.axis_index("seq")
    received = [lax.dynamic_index_in_dim(x, me, axis=0, keepdims=False)]
    for step in range(1, count):
        chunk = lax.dynamic_index_in_dim(x, (me + step) % count, axis=0, keepdims=False)
        received.append(lax.ppermute(chunk, "seq", [(j, (j + step) % count) for j in range(count)]))
    by_step = jnp.stack(received)
    return jnp.stack([jnp.take(by_step, (me - i) % count, axis=0) for i in range(count)])


def attention_by_batch(pooled, up_weight, norm_gain, qkv_weight, out_weight):
    batch_count, pooled_rows, channels = pooled.shape
    seq = lax.axis_size("seq")
    group = lax.axis_size(CHANNELS)
    per = batch_count // seq
    length = seq * pooled_rows
    mine = seq_exchange(pooled.reshape(seq, per, pooled_rows, channels))
    mine = jnp.transpose(mine, (1, 0, 2, 3)).reshape(per, length, channels)
    pooled_all = gathered_packed(mine, CHANNELS)
    up_blocks = up_weight.reshape(up_weight.shape[0], group, channels)
    hidden = jnp.einsum("nbti,oni->bto", pooled_all, up_blocks, precision=MATMUL_PRECISION)
    hidden_all = gathered_packed(hidden, CHANNELS)
    positions = jnp.arange(length, dtype=jnp.int32).astype(jnp.float32)
    query_rows, key_matrix, value_matrix = head_attention(hidden_all, norm_gain, qkv_weight, positions)
    attention_scores = jnp.einsum(
        "btc,bxc->btx", query_rows, key_matrix, precision=MATMUL_PRECISION
    )
    top = jnp.max(attention_scores, axis=2)
    probabilities = jnp.exp(attention_scores - top[..., None])
    denominator = jnp.sum(probabilities, axis=2)
    weighted_values = jnp.einsum(
        "btx,bxe->bte", probabilities, value_matrix, precision=MATMUL_PRECISION
    )
    head_result = weighted_values / denominator[..., None]
    out_width = out_weight.shape[1] // group
    out_blocks = out_weight.reshape(out_weight.shape[0], group, out_width)
    shares = jnp.einsum("btd,dne->nbte", head_result, out_blocks, precision=MATMUL_PRECISION)
    summed = jnp.sum(lax.all_to_all(shares, CHANNELS, 0, 0, tiled=True), axis=0)
    by_block = jnp.transpose(summed.reshape(per, seq, pooled_rows, out_width), (1, 0, 2, 3))
    back = seq_exchange(packed(by_block))
    return unpacked(back, pooled_rows, out_width).reshape(batch_count, pooled_rows, out_width)


def attention_by_position(pooled, up_weight, norm_gain, qkv_weight, out_weight):
    batch_count, pooled_rows, channels = pooled.shape
    group = lax.axis_size(CHANNELS)
    pooled_all = gathered_packed(pooled, CHANNELS)
    up_blocks = up_weight.reshape(up_weight.shape[0], group, channels)
    hidden = jnp.einsum("nbti,oni->bto", pooled_all, up_blocks, precision=MATMUL_PRECISION)
    hidden_all = gathered_packed(hidden, CHANNELS)
    positions = (
        lax.axis_index("seq") * pooled_rows + jnp.arange(pooled_rows, dtype=jnp.int32)
    ).astype(jnp.float32)
    query_rows, key_matrix, value_matrix = head_attention(hidden_all, norm_gain, qkv_weight, positions)
    head_extent = query_rows.shape[-1]
    keys_and_values = jnp.concatenate([key_matrix, value_matrix], axis=2)
    kv_all = gathered(keys_and_values, "seq")
    attention_scores = jnp.einsum(
        "btc,nbxc->btnx", query_rows, kv_all[..., :head_extent], precision=MATMUL_PRECISION
    )
    top = jnp.max(attention_scores, axis=(2, 3))
    probabilities = jnp.exp(attention_scores - top[..., None, None])
    denominator = jnp.sum(probabilities, axis=(2, 3))
    weighted_values = jnp.einsum(
        "btnx,nbxe->bte", probabilities, kv_all[..., head_extent:], precision=MATMUL_PRECISION
    )
    head_result = weighted_values / denominator[..., None]
    out_width = out_weight.shape[1] // group
    out_blocks = out_weight.reshape(out_weight.shape[0], group, out_width)
    shares = jnp.einsum("btd,dne->nbte", head_result, out_blocks, precision=MATMUL_PRECISION)
    summed = jnp.sum(lax.all_to_all(packed(shares), CHANNELS, 0, 0, tiled=True), axis=0)
    return unpacked(summed, pooled_rows, out_width)


def per_device(
    features,
    first_channel_scale,
    first_channel_shift,
    first_conv_bias,
    first_kernel_taps,
    second_channel_scale,
    second_channel_shift,
    second_conv_bias,
    second_kernel_taps,
    up_weight,
    norm_gain,
    qkv_weight,
    out_weight,
):
    batch_count = features.shape[0]
    channels = features.shape[1]
    row_count = features.shape[2]
    first_part = convolution_block(
        features,
        first_channel_scale,
        first_channel_shift,
        first_conv_bias,
        first_kernel_taps,
        FIRST_DILATION,
    )
    tower_skip_output = convolution_block(
        first_part,
        second_channel_scale,
        second_channel_shift,
        second_conv_bias,
        second_kernel_taps,
        SECOND_DILATION,
    )
    pooled_rows = row_count // POOL
    pooled = jnp.transpose(
        jnp.max(tower_skip_output.reshape(batch_count, channels, pooled_rows, POOL), axis=3),
        (0, 2, 1),
    )
    if batch_count % lax.axis_size("seq") == 0:
        attended = attention_by_batch(pooled, up_weight, norm_gain, qkv_weight, out_weight)
    else:
        attended = attention_by_position(pooled, up_weight, norm_gain, qkv_weight, out_weight)
    return (tower_skip_output, attended)


def solution(mesh):
    placed = (
        P(None, CHANNELS, "seq"),
        P(CHANNELS),
        P(CHANNELS),
        P(CHANNELS),
        P(None, CHANNELS, None),
        P(CHANNELS),
        P(CHANNELS),
        P(CHANNELS),
        P(None, CHANNELS, None),
        P(CHANNELS, None),
        P(),
        P(None, CHANNELS),
        P(CHANNELS, None),
    )
    return jax.shard_map(
        per_device,
        mesh=mesh,
        in_specs=placed,
        out_specs=(P(None, CHANNELS, "seq"), P(None, "seq", CHANNELS)),
        check_vma=False,
    )
```

```python
import math

import jax
import jax.numpy as jnp
from jax import lax
from jax.sharding import PartitionSpec as P

FIRST_DILATION = 2
SECOND_DILATION = 4
POOL = 8
TAPS = 5

MATMUL_PRECISION = lax.Precision.HIGH
CHANNELS = ("crow", "ccol")


def gathered(x, axis_name):
    count = lax.axis_size(axis_name)
    copies = jnp.broadcast_to(x[None], (count,) + x.shape)
    return lax.all_to_all(copies, axis_name, 0, 0, tiled=True)


def summed_scatter(x, axis_name):
    return jnp.sum(lax.all_to_all(x, axis_name, 0, 0, tiled=True), axis=0)


def swap_ccol(x):
    return lax.ppermute(x, "ccol", [(0, 1), (1, 0)])


def shifted_in(edge, forward):
    count = lax.axis_size("seq")
    if forward:
        pairs = [(i, i + 1) for i in range(count - 1)]
    else:
        pairs = [(i + 1, i) for i in range(count - 1)]
    return lax.ppermute(edge, "seq", pairs)


def row_exchange(activated):
    pairs = lambda step: [(j, j ^ step) for j in range(4)]
    across = lax.ppermute(activated, "crow", pairs(1))
    along = lax.ppermute(activated, "crow", pairs(2))
    half = activated.shape[0] // 2
    first = lax.ppermute(across[:half], "crow", pairs(2))
    second = lax.ppermute(along[half:], "crow", pairs(1))
    diagonal = jnp.concatenate([first, second], axis=0)
    slots = [activated, across, along, diagonal]
    return jnp.stack(slots), jnp.stack([swap_ccol(one) for one in slots])


def convolution_block(inputs, bn_scale, bn_shift, conv_bias, kernel, dilation):
    activated = jax.nn.gelu(inputs * bn_scale[:, None] + bn_shift[:, None], approximate=False)
    core = lax.axis_index("ccol")
    if lax.axis_size("crow") == 4 and activated.shape[0] % 2 == 0:
        slots, other_slots = row_exchange(activated)
        row = lax.axis_index("crow")
        by_row = jnp.stack([jnp.take(slots, jnp.bitwise_xor(row, r), axis=0) for r in range(4)])
        other_core = jnp.stack([jnp.take(other_slots, jnp.bitwise_xor(row, r), axis=0) for r in range(4)])
    else:
        by_row = gathered(activated, "crow")
        other_core = swap_ccol(by_row)
    tap_count, out_count, in_count = kernel.shape
    row_count, batch_count, block, rows = by_row.shape
    slot = lax.broadcasted_iota(jnp.int32, (1, 2, 1, 1, 1), 1)
    ordered = jnp.where(slot == core, by_row[:, None], other_core[:, None])
    ordered = jnp.transpose(ordered, (2, 4, 0, 1, 3)).reshape(batch_count, rows, in_count)
    products = jnp.einsum("btc,koc->kbto", ordered, kernel, precision=MATMUL_PRECISION)
    batch_count, rows = inputs.shape[0], inputs.shape[2]
    width = 2 * dilation
    padded = jnp.pad(products, ((0, 0), (0, 0), (2 * width, 2 * width), (0, 0)))
    spread = None
    for tap_index in range(tap_count):
        offset = tap_index * dilation
        term = padded[tap_index, :, offset : offset + rows + 2 * width, :]
        spread = term if spread is None else spread + term
    spread = jnp.swapaxes(spread, 1, 2)
    to_left = jnp.swapaxes(spread[..., :width], 1, 2)
    to_right = jnp.swapaxes(spread[..., rows + width :], 1, 2)
    from_left = jnp.swapaxes(shifted_in(to_right, True), 1, 2)
    from_right = jnp.swapaxes(shifted_in(to_left, False), 1, 2)
    edges = jnp.concatenate(
        [from_left, jnp.zeros((batch_count, out_count, rows - 2 * width), jnp.float32), from_right],
        axis=2,
    )
    summed = spread[..., width : width + rows] + edges
    return inputs + summed + conv_bias[:, None]


def rotate(values, positions):
    half_width = values.shape[-1] // 2
    frequency = jnp.exp(
        -math.log(10000.0) * jnp.arange(half_width).astype(jnp.float32) / half_width
    )
    angle = positions[:, None] * frequency[None, :]
    cosine = jnp.cos(angle)
    sine_part = jnp.sin(angle)
    lower_half = values[..., :half_width]
    upper_half = values[..., half_width:]
    return jnp.concatenate(
        [
            lower_half * cosine - upper_half * sine_part,
            lower_half * sine_part + upper_half * cosine,
        ],
        axis=-1,
    )


LANES = 128


def packed(x):
    rows, width = x.shape[-2:]
    if (rows * width) % LANES:
        return x
    return x.reshape(x.shape[:-2] + (rows * width // LANES, LANES))


def unpacked(x, rows, width):
    return x.reshape(x.shape[:-2] + (rows, width))


def gathered_packed(x, axis_name):
    rows, width = x.shape[-2:]
    return unpacked(gathered(packed(x), axis_name), rows, width)


def head_attention(hidden_all, norm_gain, qkv_weight, positions):
    group = hidden_all.shape[0]
    attn_width = norm_gain.shape[0]
    squares = jnp.sum(hidden_all * hidden_all, axis=(0, 3))
    gain_blocks = norm_gain.reshape(group, 1, 1, attn_width // group)
    qkv_blocks = qkv_weight.reshape(group, attn_width // group, qkv_weight.shape[1])
    projected = jnp.einsum(
        "nbtj,njo->bto", hidden_all * gain_blocks, qkv_blocks, precision=MATMUL_PRECISION
    )
    root_mean = jnp.sqrt(squares / attn_width + 1e-06)
    projected = projected / root_mean[..., None]
    head_extent = qkv_weight.shape[1] // 3
    query_rows = rotate(projected[..., :head_extent], positions) / math.sqrt(head_extent)
    key_matrix = rotate(projected[..., head_extent : 2 * head_extent], positions)
    return query_rows, key_matrix, projected[..., 2 * head_extent :]


def attention_by_batch(pooled, up_weight, norm_gain, qkv_weight, out_weight):
    batch_count, pooled_rows, channels = pooled.shape
    seq = lax.axis_size("seq")
    group = lax.axis_size(CHANNELS)
    per = batch_count // seq
    length = seq * pooled_rows
    mine = lax.all_to_all(pooled.reshape(seq, per, pooled_rows, channels), "seq", 0, 0, tiled=True)
    mine = jnp.transpose(mine, (1, 0, 2, 3)).reshape(per, length, channels)
    pooled_all = gathered_packed(mine, CHANNELS)
    up_blocks = up_weight.reshape(up_weight.shape[0], group, channels)
    hidden = jnp.einsum("nbti,oni->bto", pooled_all, up_blocks, precision=MATMUL_PRECISION)
    hidden_all = gathered_packed(hidden, CHANNELS)
    positions = jnp.arange(length, dtype=jnp.int32).astype(jnp.float32)
    query_rows, key_matrix, value_matrix = head_attention(hidden_all, norm_gain, qkv_weight, positions)
    attention_scores = jnp.einsum(
        "btc,bxc->btx", query_rows, key_matrix, precision=MATMUL_PRECISION
    )
    top = jnp.max(attention_scores, axis=2)
    probabilities = jnp.exp(attention_scores - top[..., None])
    denominator = jnp.sum(probabilities, axis=2)
    weighted_values = jnp.einsum(
        "btx,bxe->bte", probabilities, value_matrix, precision=MATMUL_PRECISION
    )
    head_result = weighted_values / denominator[..., None]
    out_width = out_weight.shape[1] // group
    out_blocks = out_weight.reshape(out_weight.shape[0], group, out_width)
    shares = jnp.einsum("btd,dne->nbet", head_result, out_blocks, precision=MATMUL_PRECISION)
    summed = jnp.swapaxes(jnp.sum(lax.all_to_all(shares, CHANNELS, 0, 0, tiled=True), axis=0), 1, 2)
    by_block = jnp.transpose(summed.reshape(per, seq, pooled_rows, out_width), (1, 0, 2, 3))
    back = lax.all_to_all(packed(by_block), "seq", 0, 0, tiled=True)
    return unpacked(back, pooled_rows, out_width).reshape(batch_count, pooled_rows, out_width)


def attention_by_position(pooled, up_weight, norm_gain, qkv_weight, out_weight):
    batch_count, pooled_rows, channels = pooled.shape
    group = lax.axis_size(CHANNELS)
    pooled_all = gathered_packed(pooled, CHANNELS)
    up_blocks = up_weight.reshape(up_weight.shape[0], group, channels)
    hidden = jnp.einsum("nbti,oni->bto", pooled_all, up_blocks, precision=MATMUL_PRECISION)
    hidden_all = gathered_packed(hidden, CHANNELS)
    positions = (
        lax.axis_index("seq") * pooled_rows + jnp.arange(pooled_rows, dtype=jnp.int32)
    ).astype(jnp.float32)
    query_rows, key_matrix, value_matrix = head_attention(hidden_all, norm_gain, qkv_weight, positions)
    head_extent = query_rows.shape[-1]
    keys_and_values = jnp.concatenate([key_matrix, value_matrix], axis=2)
    kv_all = gathered(keys_and_values, "seq")
    attention_scores = jnp.einsum(
        "btc,nbxc->btnx", query_rows, kv_all[..., :head_extent], precision=MATMUL_PRECISION
    )
    top = jnp.max(attention_scores, axis=(2, 3))
    probabilities = jnp.exp(attention_scores - top[..., None, None])
    denominator = jnp.sum(probabilities, axis=(2, 3))
    weighted_values = jnp.einsum(
        "btnx,nbxe->bte", probabilities, kv_all[..., head_extent:], precision=MATMUL_PRECISION
    )
    head_result = weighted_values / denominator[..., None]
    out_width = out_weight.shape[1] // group
    out_blocks = out_weight.reshape(out_weight.shape[0], group, out_width)
    shares = jnp.einsum("btd,dne->nbte", head_result, out_blocks, precision=MATMUL_PRECISION)
    summed = jnp.sum(lax.all_to_all(packed(shares), CHANNELS, 0, 0, tiled=True), axis=0)
    return unpacked(summed, pooled_rows, out_width)


def per_device(
    features,
    first_channel_scale,
    first_channel_shift,
    first_conv_bias,
    first_kernel_taps,
    second_channel_scale,
    second_channel_shift,
    second_conv_bias,
    second_kernel_taps,
    up_weight,
    norm_gain,
    qkv_weight,
    out_weight,
):
    batch_count = features.shape[0]
    channels = features.shape[1]
    row_count = features.shape[2]
    first_part = convolution_block(
        features,
        first_channel_scale,
        first_channel_shift,
        first_conv_bias,
        first_kernel_taps,
        FIRST_DILATION,
    )
    tower_skip_output = convolution_block(
        first_part,
        second_channel_scale,
        second_channel_shift,
        second_conv_bias,
        second_kernel_taps,
        SECOND_DILATION,
    )
    pooled_rows = row_count // POOL
    pooled = jnp.transpose(
        jnp.max(tower_skip_output.reshape(batch_count, channels, pooled_rows, POOL), axis=3),
        (0, 2, 1),
    )
    if batch_count % lax.axis_size("seq") == 0:
        attended = attention_by_batch(pooled, up_weight, norm_gain, qkv_weight, out_weight)
    else:
        attended = attention_by_position(pooled, up_weight, norm_gain, qkv_weight, out_weight)
    return (tower_skip_output, attended)


def solution(mesh):
    placed = (
        P(None, CHANNELS, "seq"),
        P(CHANNELS),
        P(CHANNELS),
        P(CHANNELS),
        P(None, CHANNELS, None),
        P(CHANNELS),
        P(CHANNELS),
        P(CHANNELS),
        P(None, CHANNELS, None),
        P(CHANNELS, None),
        P(),
        P(None, CHANNELS),
        P(CHANNELS, None),
    )
    return jax.shard_map(
        per_device,
        mesh=mesh,
        in_specs=placed,
        out_specs=(P(None, CHANNELS, "seq"), P(None, "seq", CHANNELS)),
        check_vma=False,
    )
```

```python
import math

import jax
import jax.numpy as jnp
from jax import lax
from jax.sharding import PartitionSpec as P

FIRST_DILATION = 2
SECOND_DILATION = 4
POOL = 8
TAPS = 5

MATMUL_PRECISION = lax.Precision.HIGH
CHANNELS = ("crow", "ccol")


def gathered(x, axis_name):
    count = lax.axis_size(axis_name)
    copies = jnp.broadcast_to(x[None], (count,) + x.shape)
    return lax.all_to_all(copies, axis_name, 0, 0, tiled=True)


def summed_scatter(x, axis_name):
    return jnp.sum(lax.all_to_all(x, axis_name, 0, 0, tiled=True), axis=0)


def swap_ccol(x):
    return lax.ppermute(x, "ccol", [(0, 1), (1, 0)])


def shifted_in(edge, forward):
    count = lax.axis_size("seq")
    if forward:
        pairs = [(i, i + 1) for i in range(count - 1)]
    else:
        pairs = [(i + 1, i) for i in range(count - 1)]
    return lax.ppermute(edge, "seq", pairs)


def row_exchange(activated):
    pairs = lambda step: [(j, j ^ step) for j in range(4)]
    across = lax.ppermute(activated, "crow", pairs(1))
    along = lax.ppermute(activated, "crow", pairs(2))
    half = activated.shape[0] // 2
    first = lax.ppermute(across[:half], "crow", pairs(2))
    second = lax.ppermute(along[half:], "crow", pairs(1))
    diagonal = jnp.concatenate([first, second], axis=0)
    slots = [activated, across, along, diagonal]
    return jnp.stack(slots), jnp.stack([swap_ccol(one) for one in slots])


def convolution_block(inputs, bn_scale, bn_shift, conv_bias, kernel, dilation):
    activated = jax.nn.gelu(inputs * bn_scale[:, None] + bn_shift[:, None], approximate=False)
    core = lax.axis_index("ccol")
    if lax.axis_size("crow") == 4 and activated.shape[0] % 2 == 0:
        slots, other_slots = row_exchange(activated)
        row = lax.axis_index("crow")
        by_row = jnp.stack([jnp.take(slots, jnp.bitwise_xor(row, r), axis=0) for r in range(4)])
        other_core = jnp.stack([jnp.take(other_slots, jnp.bitwise_xor(row, r), axis=0) for r in range(4)])
    else:
        by_row = gathered(activated, "crow")
        other_core = swap_ccol(by_row)
    tap_count, out_count, in_count = kernel.shape
    row_count, batch_count, block, rows = by_row.shape
    slot = lax.broadcasted_iota(jnp.int32, (1, 2, 1, 1, 1), 1)
    ordered = jnp.where(slot == core, by_row[:, None], other_core[:, None])
    ordered = jnp.transpose(ordered, (2, 4, 0, 1, 3)).reshape(batch_count, rows, in_count)
    products = jnp.einsum("btc,koc->kbto", ordered, kernel, precision=MATMUL_PRECISION)
    batch_count, rows = inputs.shape[0], inputs.shape[2]
    width = 2 * dilation
    padded = jnp.pad(products, ((0, 0), (0, 0), (2 * width, 2 * width), (0, 0)))
    spread = None
    for tap_index in range(tap_count):
        offset = tap_index * dilation
        term = padded[tap_index, :, offset : offset + rows + 2 * width, :]
        spread = term if spread is None else spread + term
    spread = jnp.swapaxes(spread, 1, 2)
    to_left = sum(
        padded[k, :, k * dilation : k * dilation + width, :] for k in range(tap_count)
    )
    to_right = sum(
        padded[k, :, k * dilation + rows + width : k * dilation + rows + 2 * width, :]
        for k in range(tap_count)
    )
    from_left = jnp.swapaxes(shifted_in(to_right, True), 1, 2)
    from_right = jnp.swapaxes(shifted_in(to_left, False), 1, 2)
    edges = jnp.concatenate(
        [from_left, jnp.zeros((batch_count, out_count, rows - 2 * width), jnp.float32), from_right],
        axis=2,
    )
    summed = spread[..., width : width + rows] + edges
    return inputs + summed + conv_bias[:, None]


def rotate(values, positions):
    half_width = values.shape[-1] // 2
    frequency = jnp.exp(
        -math.log(10000.0) * jnp.arange(half_width).astype(jnp.float32) / half_width
    )
    angle = positions[:, None] * frequency[None, :]
    cosine = jnp.cos(angle)
    sine_part = jnp.sin(angle)
    lower_half = values[..., :half_width]
    upper_half = values[..., half_width:]
    return jnp.concatenate(
        [
            lower_half * cosine - upper_half * sine_part,
            lower_half * sine_part + upper_half * cosine,
        ],
        axis=-1,
    )


LANES = 128


def packed(x):
    rows, width = x.shape[-2:]
    if (rows * width) % LANES:
        return x
    return x.reshape(x.shape[:-2] + (rows * width // LANES, LANES))


def unpacked(x, rows, width):
    return x.reshape(x.shape[:-2] + (rows, width))


def gathered_packed(x, axis_name):
    rows, width = x.shape[-2:]
    return unpacked(gathered(packed(x), axis_name), rows, width)


def head_attention(hidden_all, norm_gain, qkv_weight, positions):
    group = hidden_all.shape[0]
    attn_width = norm_gain.shape[0]
    squares = jnp.sum(hidden_all * hidden_all, axis=(0, 3))
    gain_blocks = norm_gain.reshape(group, 1, 1, attn_width // group)
    qkv_blocks = qkv_weight.reshape(group, attn_width // group, qkv_weight.shape[1])
    projected = jnp.einsum(
        "nbtj,njo->bto", hidden_all * gain_blocks, qkv_blocks, precision=MATMUL_PRECISION
    )
    root_mean = jnp.sqrt(squares / attn_width + 1e-06)
    projected = projected / root_mean[..., None]
    head_extent = qkv_weight.shape[1] // 3
    query_rows = rotate(projected[..., :head_extent], positions) / math.sqrt(head_extent)
    key_matrix = rotate(projected[..., head_extent : 2 * head_extent], positions)
    return query_rows, key_matrix, projected[..., 2 * head_extent :]


def attention_by_batch(pooled, up_weight, norm_gain, qkv_weight, out_weight):
    batch_count, pooled_rows, channels = pooled.shape
    seq = lax.axis_size("seq")
    group = lax.axis_size(CHANNELS)
    per = batch_count // seq
    length = seq * pooled_rows
    mine = lax.all_to_all(pooled.reshape(seq, per, pooled_rows, channels), "seq", 0, 0, tiled=True)
    mine = jnp.transpose(mine, (1, 0, 2, 3)).reshape(per, length, channels)
    pooled_all = gathered_packed(mine, CHANNELS)
    up_blocks = up_weight.reshape(up_weight.shape[0], group, channels)
    hidden = jnp.einsum("nbti,oni->bto", pooled_all, up_blocks, precision=MATMUL_PRECISION)
    hidden_all = gathered_packed(hidden, CHANNELS)
    positions = jnp.arange(length, dtype=jnp.int32).astype(jnp.float32)
    query_rows, key_matrix, value_matrix = head_attention(hidden_all, norm_gain, qkv_weight, positions)
    attention_scores = jnp.einsum(
        "btc,bxc->btx", query_rows, key_matrix, precision=MATMUL_PRECISION
    )
    top = jnp.max(attention_scores, axis=2)
    probabilities = jnp.exp(attention_scores - top[..., None])
    denominator = jnp.sum(probabilities, axis=2)
    weighted_values = jnp.einsum(
        "btx,bxe->bte", probabilities, value_matrix, precision=MATMUL_PRECISION
    )
    head_result = weighted_values / denominator[..., None]
    out_width = out_weight.shape[1] // group
    out_blocks = out_weight.reshape(out_weight.shape[0], group, out_width)
    shares = jnp.einsum("btd,dne->nbte", head_result, out_blocks, precision=MATMUL_PRECISION)
    summed = jnp.sum(lax.all_to_all(shares, CHANNELS, 0, 0, tiled=True), axis=0)
    by_block = jnp.transpose(summed.reshape(per, seq, pooled_rows, out_width), (1, 0, 2, 3))
    back = lax.all_to_all(packed(by_block), "seq", 0, 0, tiled=True)
    return unpacked(back, pooled_rows, out_width).reshape(batch_count, pooled_rows, out_width)


def attention_by_position(pooled, up_weight, norm_gain, qkv_weight, out_weight):
    batch_count, pooled_rows, channels = pooled.shape
    group = lax.axis_size(CHANNELS)
    pooled_all = gathered_packed(pooled, CHANNELS)
    up_blocks = up_weight.reshape(up_weight.shape[0], group, channels)
    hidden = jnp.einsum("nbti,oni->bto", pooled_all, up_blocks, precision=MATMUL_PRECISION)
    hidden_all = gathered_packed(hidden, CHANNELS)
    positions = (
        lax.axis_index("seq") * pooled_rows + jnp.arange(pooled_rows, dtype=jnp.int32)
    ).astype(jnp.float32)
    query_rows, key_matrix, value_matrix = head_attention(hidden_all, norm_gain, qkv_weight, positions)
    head_extent = query_rows.shape[-1]
    keys_and_values = jnp.concatenate([key_matrix, value_matrix], axis=2)
    kv_all = gathered(keys_and_values, "seq")
    attention_scores = jnp.einsum(
        "btc,nbxc->btnx", query_rows, kv_all[..., :head_extent], precision=MATMUL_PRECISION
    )
    top = jnp.max(attention_scores, axis=(2, 3))
    probabilities = jnp.exp(attention_scores - top[..., None, None])
    denominator = jnp.sum(probabilities, axis=(2, 3))
    weighted_values = jnp.einsum(
        "btnx,nbxe->bte", probabilities, kv_all[..., head_extent:], precision=MATMUL_PRECISION
    )
    head_result = weighted_values / denominator[..., None]
    out_width = out_weight.shape[1] // group
    out_blocks = out_weight.reshape(out_weight.shape[0], group, out_width)
    shares = jnp.einsum("btd,dne->nbte", head_result, out_blocks, precision=MATMUL_PRECISION)
    summed = jnp.sum(lax.all_to_all(packed(shares), CHANNELS, 0, 0, tiled=True), axis=0)
    return unpacked(summed, pooled_rows, out_width)


def per_device(
    features,
    first_channel_scale,
    first_channel_shift,
    first_conv_bias,
    first_kernel_taps,
    second_channel_scale,
    second_channel_shift,
    second_conv_bias,
    second_kernel_taps,
    up_weight,
    norm_gain,
    qkv_weight,
    out_weight,
):
    batch_count = features.shape[0]
    channels = features.shape[1]
    row_count = features.shape[2]
    first_part = convolution_block(
        features,
        first_channel_scale,
        first_channel_shift,
        first_conv_bias,
        first_kernel_taps,
        FIRST_DILATION,
    )
    tower_skip_output = convolution_block(
        first_part,
        second_channel_scale,
        second_channel_shift,
        second_conv_bias,
        second_kernel_taps,
        SECOND_DILATION,
    )
    pooled_rows = row_count // POOL
    pooled = jnp.transpose(
        jnp.max(tower_skip_output.reshape(batch_count, channels, pooled_rows, POOL), axis=3),
        (0, 2, 1),
    )
    if batch_count % lax.axis_size("seq") == 0:
        attended = attention_by_batch(pooled, up_weight, norm_gain, qkv_weight, out_weight)
    else:
        attended = attention_by_position(pooled, up_weight, norm_gain, qkv_weight, out_weight)
    return (tower_skip_output, attended)


def solution(mesh):
    placed = (
        P(None, CHANNELS, "seq"),
        P(CHANNELS),
        P(CHANNELS),
        P(CHANNELS),
        P(None, CHANNELS, None),
        P(CHANNELS),
        P(CHANNELS),
        P(CHANNELS),
        P(None, CHANNELS, None),
        P(CHANNELS, None),
        P(),
        P(None, CHANNELS),
        P(CHANNELS, None),
    )
    return jax.shard_map(
        per_device,
        mesh=mesh,
        in_specs=placed,
        out_specs=(P(None, CHANNELS, "seq"), P(None, "seq", CHANNELS)),
        check_vma=False,
    )
```

```python
import math

import jax
import jax.numpy as jnp
from jax import lax
from jax.sharding import PartitionSpec as P

FIRST_DILATION = 2
SECOND_DILATION = 4
POOL = 8
TAPS = 5

MATMUL_PRECISION = lax.Precision.HIGH
CHANNELS = ("crow", "ccol")


def gathered(x, axis_name):
    count = lax.axis_size(axis_name)
    copies = jnp.broadcast_to(x[None], (count,) + x.shape)
    return lax.all_to_all(copies, axis_name, 0, 0, tiled=True)


def summed_scatter(x, axis_name):
    return jnp.sum(lax.all_to_all(x, axis_name, 0, 0, tiled=True), axis=0)


def swap_ccol(x):
    return lax.ppermute(x, "ccol", [(0, 1), (1, 0)])


def shifted_in(edge, forward):
    count = lax.axis_size("seq")
    if forward:
        pairs = [(i, i + 1) for i in range(count - 1)]
    else:
        pairs = [(i + 1, i) for i in range(count - 1)]
    return lax.ppermute(edge, "seq", pairs)


def row_exchange(activated):
    pairs = lambda step: [(j, j ^ step) for j in range(4)]
    across = lax.ppermute(activated, "crow", pairs(1))
    along = lax.ppermute(activated, "crow", pairs(2))
    half = activated.shape[0] // 2
    first = lax.ppermute(across[:half], "crow", pairs(2))
    second = lax.ppermute(along[half:], "crow", pairs(1))
    diagonal = jnp.concatenate([first, second], axis=0)
    slots = [activated, across, along, diagonal]
    return jnp.stack(slots), jnp.stack([swap_ccol(one) for one in slots])


def convolution_block(inputs, bn_scale, bn_shift, conv_bias, kernel, dilation):
    activated = jax.nn.gelu(inputs * bn_scale[:, None] + bn_shift[:, None], approximate=False)
    core = lax.axis_index("ccol")
    if lax.axis_size("crow") == 4 and activated.shape[0] % 2 == 0:
        slots, other_slots = row_exchange(activated)
        row = lax.axis_index("crow")
        by_row = jnp.stack([jnp.take(slots, jnp.bitwise_xor(row, r), axis=0) for r in range(4)])
        other_core = jnp.stack([jnp.take(other_slots, jnp.bitwise_xor(row, r), axis=0) for r in range(4)])
    else:
        by_row = gathered(activated, "crow")
        other_core = swap_ccol(by_row)
    tap_count, out_count, in_count = kernel.shape
    row_count, batch_count, block, rows = by_row.shape
    slot = lax.broadcasted_iota(jnp.int32, (1, 2, 1, 1, 1), 1)
    ordered = jnp.where(slot == core, by_row[:, None], other_core[:, None])
    ordered = jnp.transpose(ordered, (2, 4, 0, 1, 3)).reshape(batch_count, rows, in_count)
    products = jnp.einsum("btc,koc->kbto", ordered, kernel, precision=MATMUL_PRECISION)
    batch_count, rows = inputs.shape[0], inputs.shape[2]
    width = 2 * dilation
    padded = jnp.pad(products, ((0, 0), (0, 0), (2 * width, 2 * width), (0, 0)))
    spread = None
    for tap_index in range(tap_count):
        offset = tap_index * dilation
        term = padded[tap_index, :, offset : offset + rows + 2 * width, :]
        spread = term if spread is None else spread + term
    spread = jnp.swapaxes(spread, 1, 2)
    to_left = jnp.swapaxes(spread[..., :width], 1, 2)
    to_right = jnp.swapaxes(spread[..., rows + width :], 1, 2)
    from_left = jnp.swapaxes(shifted_in(to_right, True), 1, 2)
    from_right = jnp.swapaxes(shifted_in(to_left, False), 1, 2)
    edges = jnp.concatenate(
        [from_left, jnp.zeros((batch_count, out_count, rows - 2 * width), jnp.float32), from_right],
        axis=2,
    )
    summed = spread[..., width : width + rows] + edges
    return inputs + summed + conv_bias[:, None]


def rotate(values, positions):
    half_width = values.shape[-1] // 2
    frequency = jnp.exp(
        -math.log(10000.0) * jnp.arange(half_width).astype(jnp.float32) / half_width
    )
    angle = positions[:, None] * frequency[None, :]
    cosine = jnp.cos(angle)
    sine_part = jnp.sin(angle)
    lower_half = values[..., :half_width]
    upper_half = values[..., half_width:]
    return jnp.concatenate(
        [
            lower_half * cosine - upper_half * sine_part,
            lower_half * sine_part + upper_half * cosine,
        ],
        axis=-1,
    )


LANES = 128


def packed(x):
    rows, width = x.shape[-2:]
    if (rows * width) % LANES:
        return x
    return x.reshape(x.shape[:-2] + (rows * width // LANES, LANES))


def unpacked(x, rows, width):
    return x.reshape(x.shape[:-2] + (rows, width))


def gathered_packed(x, axis_name):
    rows, width = x.shape[-2:]
    return unpacked(gathered(packed(x), axis_name), rows, width)


def head_attention(hidden_all, norm_gain, qkv_weight, positions):
    group = hidden_all.shape[0]
    attn_width = norm_gain.shape[0]
    squares = jnp.sum(hidden_all * hidden_all, axis=(0, 3))
    gain_blocks = norm_gain.reshape(group, 1, 1, attn_width // group)
    qkv_blocks = qkv_weight.reshape(group, attn_width // group, qkv_weight.shape[1])
    projected = jnp.einsum(
        "nbtj,njo->bto", hidden_all * gain_blocks, qkv_blocks, precision=MATMUL_PRECISION
    )
    root_mean = jnp.sqrt(squares / attn_width + 1e-06)
    projected = projected / root_mean[..., None]
    head_extent = qkv_weight.shape[1] // 3
    query_rows = rotate(projected[..., :head_extent], positions) / math.sqrt(head_extent)
    key_matrix = rotate(projected[..., head_extent : 2 * head_extent], positions)
    return query_rows, key_matrix, projected[..., 2 * head_extent :]


def attention_by_batch(pooled, up_weight, norm_gain, qkv_weight, out_weight):
    batch_count, pooled_rows, channels = pooled.shape
    seq = lax.axis_size("seq")
    group = lax.axis_size(CHANNELS)
    per = batch_count // seq
    length = seq * pooled_rows
    mine = lax.all_to_all(pooled.reshape(seq, per, pooled_rows, channels), "seq", 0, 0, tiled=True)
    mine = jnp.transpose(mine, (1, 0, 2, 3)).reshape(per, length, channels)
    pooled_all = gathered(mine, CHANNELS)
    up_blocks = up_weight.reshape(up_weight.shape[0], group, channels)
    hidden = jnp.einsum("nbti,oni->bto", pooled_all, up_blocks, precision=MATMUL_PRECISION)
    hidden_all = gathered_packed(hidden, CHANNELS)
    positions = jnp.arange(length, dtype=jnp.int32).astype(jnp.float32)
    query_rows, key_matrix, value_matrix = head_attention(hidden_all, norm_gain, qkv_weight, positions)
    attention_scores = jnp.einsum(
        "btc,bxc->btx", query_rows, key_matrix, precision=MATMUL_PRECISION
    )
    top = jnp.max(attention_scores, axis=2)
    probabilities = jnp.exp(attention_scores - top[..., None])
    denominator = jnp.sum(probabilities, axis=2)
    weighted_values = jnp.einsum(
        "btx,bxe->bte", probabilities, value_matrix, precision=MATMUL_PRECISION
    )
    head_result = weighted_values / denominator[..., None]
    out_width = out_weight.shape[1] // group
    out_blocks = out_weight.reshape(out_weight.shape[0], group, out_width)
    shares = jnp.einsum("btd,dne->nbte", head_result, out_blocks, precision=MATMUL_PRECISION)
    summed = jnp.sum(lax.all_to_all(shares, CHANNELS, 0, 0, tiled=True), axis=0)
    by_block = jnp.transpose(summed.reshape(per, seq, pooled_rows, out_width), (1, 0, 2, 3))
    back = lax.all_to_all(packed(by_block), "seq", 0, 0, tiled=True)
    return unpacked(back, pooled_rows, out_width).reshape(batch_count, pooled_rows, out_width)


def attention_by_position(pooled, up_weight, norm_gain, qkv_weight, out_weight):
    batch_count, pooled_rows, channels = pooled.shape
    group = lax.axis_size(CHANNELS)
    pooled_all = gathered_packed(pooled, CHANNELS)
    up_blocks = up_weight.reshape(up_weight.shape[0], group, channels)
    hidden = jnp.einsum("nbti,oni->bto", pooled_all, up_blocks, precision=MATMUL_PRECISION)
    hidden_all = gathered_packed(hidden, CHANNELS)
    positions = (
        lax.axis_index("seq") * pooled_rows + jnp.arange(pooled_rows, dtype=jnp.int32)
    ).astype(jnp.float32)
    query_rows, key_matrix, value_matrix = head_attention(hidden_all, norm_gain, qkv_weight, positions)
    head_extent = query_rows.shape[-1]
    keys_and_values = jnp.concatenate([key_matrix, value_matrix], axis=2)
    kv_all = gathered(keys_and_values, "seq")
    attention_scores = jnp.einsum(
        "btc,nbxc->btnx", query_rows, kv_all[..., :head_extent], precision=MATMUL_PRECISION
    )
    top = jnp.max(attention_scores, axis=(2, 3))
    probabilities = jnp.exp(attention_scores - top[..., None, None])
    denominator = jnp.sum(probabilities, axis=(2, 3))
    weighted_values = jnp.einsum(
        "btnx,nbxe->bte", probabilities, kv_all[..., head_extent:], precision=MATMUL_PRECISION
    )
    head_result = weighted_values / denominator[..., None]
    out_width = out_weight.shape[1] // group
    out_blocks = out_weight.reshape(out_weight.shape[0], group, out_width)
    shares = jnp.einsum("btd,dne->nbte", head_result, out_blocks, precision=MATMUL_PRECISION)
    summed = jnp.sum(lax.all_to_all(packed(shares), CHANNELS, 0, 0, tiled=True), axis=0)
    return unpacked(summed, pooled_rows, out_width)


def per_device(
    features,
    first_channel_scale,
    first_channel_shift,
    first_conv_bias,
    first_kernel_taps,
    second_channel_scale,
    second_channel_shift,
    second_conv_bias,
    second_kernel_taps,
    up_weight,
    norm_gain,
    qkv_weight,
    out_weight,
):
    batch_count = features.shape[0]
    channels = features.shape[1]
    row_count = features.shape[2]
    first_part = convolution_block(
        features,
        first_channel_scale,
        first_channel_shift,
        first_conv_bias,
        first_kernel_taps,
        FIRST_DILATION,
    )
    tower_skip_output = convolution_block(
        first_part,
        second_channel_scale,
        second_channel_shift,
        second_conv_bias,
        second_kernel_taps,
        SECOND_DILATION,
    )
    pooled_rows = row_count // POOL
    pooled = jnp.transpose(
        jnp.max(tower_skip_output.reshape(batch_count, channels, pooled_rows, POOL), axis=3),
        (0, 2, 1),
    )
    if batch_count % lax.axis_size("seq") == 0:
        attended = attention_by_batch(pooled, up_weight, norm_gain, qkv_weight, out_weight)
    else:
        attended = attention_by_position(pooled, up_weight, norm_gain, qkv_weight, out_weight)
    return (tower_skip_output, attended)


def solution(mesh):
    placed = (
        P(None, CHANNELS, "seq"),
        P(CHANNELS),
        P(CHANNELS),
        P(CHANNELS),
        P(None, CHANNELS, None),
        P(CHANNELS),
        P(CHANNELS),
        P(CHANNELS),
        P(None, CHANNELS, None),
        P(CHANNELS, None),
        P(),
        P(None, CHANNELS),
        P(CHANNELS, None),
    )
    return jax.shard_map(
        per_device,
        mesh=mesh,
        in_specs=placed,
        out_specs=(P(None, CHANNELS, "seq"), P(None, "seq", CHANNELS)),
        check_vma=False,
    )
```
